256 devices in a mesh: seq: 32 (over x, z), row: 2 (over core), col: 4 (over y).
Axes of the slice: x: 4, y: 4, z: 8, core: 2. Of those that a mesh axis runs over, the one named last changes fastest.
Arguments:
- hidden: bfloat16 [16384, 4096], P(('seq', 'row'), 'col'), may hold values from -6 to 6
- w_x: bfloat16 [4096, 4, 1024], P('col', None, 'row'), may hold values from -0.09375 to 0.09375
- w_z: bfloat16 [4096, 4, 1024], P('col', None, 'row'), may hold values from -0.09375 to 0.09375
- w_bc: bfloat16 [4096, 4, 256], P('col'), may hold values from -0.09375 to 0.09375
- w_dt: bfloat16 [4096, 4, 16], P('col', None, 'row'), may hold values from -0.09375 to 0.09375
- conv_x_w: bfloat16 [4, 4, 1024], P(None, 'col', 'row'), may hold values from -3 to 3
- conv_bc_w: bfloat16 [4, 4, 256], P(None, 'col'), may hold values from -3 to 3
- conv_x_bias: bfloat16 [4, 1024], P('col', 'row'), may hold values from -3 to 3
- conv_bc_bias: bfloat16 [4, 256], P('col'), may hold values from -3 to 3
- dt_bias: float32 [4, 16], P('col', 'row'), may hold values from -5 to -2
- decay_rate: float32 [4, 16], P('col', 'row'), may hold values from 0.005 to 2
- d_skip: float32 [4, 16], P('col', 'row'), may hold values from 0.5 to 1.5
- norm_gain: float32 [4, 1024], P('col', 'row'), may hold values from 0.5 to 1.5
- starts: int32 [16384], P('seq'), may hold values from 0 to 1, as said below
- init_states: float32 [96, 4, 16, 64, 128], P('seq', 'col', 'row'), may hold values from -1.2 to 1.2
- conv_x_edges: bfloat16 [96, 3, 4, 1024], P('seq', None, 'col', 'row'), may hold values from -6 to 6
- conv_bc_edges: bfloat16 [96, 3, 4, 256], P('seq', None, 'col'), may hold values from -6 to 6
Outputs:
- gated_out: bfloat16 [16384, 4, 1024], P('seq', 'col', 'row')
- final_states: float32 [96, 4, 16, 64, 128], P('seq', 'col', 'row')
The draws below stay inside these ranges and needn't reach their ends.
Inputs may be any that keep to these rules, and one draw needn't show every extreme that they name: The first token of all has starts 1. The 512 tokens of one index of seq hold at most 3 ones, and some index holds exactly 3. The last two indices of seq each hold one or more ones. Slot j of an index of seq in init_states, conv_x_edges, conv_bc_edges and final_states belongs to the j-th request that begins among its tokens; the others are not read.
All inputs are finite; a program needn't handle non-finite values.
Results may differ from the reference program's by a relative error of at most 0.0057.
Values may be sent and summed in bfloat16 or wider, within the bound.
No kernel may reach another device: no remote copies, remote signals or barrier semaphores. Data moves between devices by JAX's collectives and lax.ppermute only.
A program may use at most 128 MiB of HBM per device.

```python
import math
import jax
import jax.numpy as jnp
from jax import lax

D = 4096
G = 4
HG = 16
P_SIZE = 64
N = 128
KCONV = 4
SLOTS = 3
TOK_DEV = 512
TOKENS = 16384
SLOTS_ALL = 96
N_SEQ = 32


def draw_starts(key, part):
    blocks = TOKENS // TOK_DEV
    key_count, key_force, key_order, key_first, key_span, key_place = jax.random.split(key, 6)
    counts = jnp.clip(jax.random.randint(key_count, (blocks,), -1, SLOTS + 1), 0, SLOTS).astype(jnp.int32)
    span_lo = max(1, min(blocks // 2, blocks - 3))
    span = jax.random.randint(key_span, (), span_lo, blocks - 2).astype(jnp.int32)
    begin = jax.random.randint(key_place, (), 1, blocks - 1 - span).astype(jnp.int32)
    block_ids = jnp.arange(blocks, dtype=jnp.int32)
    quiet = (block_ids >= begin) & (block_ids < begin + span)
    counts = jnp.where(quiet, 0, counts).astype(jnp.int32)
    outside = jax.random.randint(key_force, (), 0, blocks - span).astype(jnp.int32)
    forced = jnp.where(outside < begin, outside, outside + span).astype(jnp.int32)
    counts = jnp.where(block_ids == forced, SLOTS, counts).astype(jnp.int32)
    counts = jnp.where(block_ids >= blocks - 2, jnp.maximum(counts, 1), counts).astype(jnp.int32)
    counts = counts.at[0].set(jnp.maximum(counts[0], 1))
    order_keys = jax.random.split(key_order, blocks)
    orders = jax.vmap(lambda single: jax.random.permutation(single, TOK_DEV))(order_keys).astype(jnp.int32)
    first_row = jnp.concatenate([jnp.full((1,), -1, jnp.int32), jax.random.permutation(key_first, TOK_DEV - 1).astype(jnp.int32)])
    orders = orders.at[0].set(first_row)
    limits = counts.at[0].add(-1)
    marked = (orders < limits[:, None]).astype(jnp.int32)
    return marked.reshape(TOKENS)


def shard_levels(key, extent, shards, smallest, high):
    gain = 1.0
    for axis_at, blocks in shards:
        draws = jax.random.uniform(jax.random.fold_in(jax.random.fold_in(key, 6), axis_at), (blocks,), jnp.float32, smallest / len(shards), high / len(shards))
        gain = gain * jnp.repeat(jnp.exp(draws), extent[axis_at] // blocks).reshape((-1,) + (1,) * (len(extent) - 1 - axis_at))
    return gain


def noise(key, shape, scale, bound, cuts=(), held_as=jnp.bfloat16):
    entries = jax.random.normal(key, shape, jnp.float32) * scale
    if len(cuts) > 0:
        entries = shard_levels(key, shape, cuts, -0.22, 0.18) * entries
    return jnp.clip(entries, min=-bound, max=bound).astype(held_as)


def setup_inputs(seed: int = 0) -> dict:
    splits = jax.random.split(jax.random.key(seed), 18)
    hidden = noise(splits[0], (TOKENS, D), 1.0, 6.0, ((0, 64), (1, 4)))
    w_x = noise(splits[1], (D, G, HG * P_SIZE), D ** -0.5, 0.09375, ((0, 4), (2, 2)))
    w_z = noise(splits[2], (D, G, HG * P_SIZE), D ** -0.5, 0.09375, ((0, 4), (2, 2)))
    w_bc = noise(splits[3], (D, G, 2 * N), D ** -0.5, 0.09375, ((0, 4),))
    w_dt = noise(splits[4], (D, G, HG), D ** -0.5, 0.09375, ((0, 4), (2, 2)))
    conv_x_w = noise(splits[5], (KCONV, G, HG * P_SIZE), 0.5, 3.0, ((1, 4), (2, 2)))
    conv_bc_w = noise(splits[6], (KCONV, G, 2 * N), 0.5, 3.0, ((1, 4),))
    conv_x_bias = noise(splits[7], (G, HG * P_SIZE), 0.5, 3.0, ((0, 4), (1, 2)))
    conv_bc_bias = noise(splits[8], (G, 2 * N), 0.5, 3.0, ((0, 4),))
    dt_bias = jnp.clip(-5.0 + 3.0 * jax.random.uniform(splits[9], (G, HG), jnp.float32) ** shard_levels(splits[9], (G, HG), ((0, 4), (1, 2)), -0.2, 0.2), -5.0, -2.0)
    decay_rate = jnp.clip(jnp.exp(math.log(2.0) - 5.9914646 * jax.random.uniform(splits[10], (G, HG), jnp.float32) ** shard_levels(splits[10], (G, HG), ((0, 4), (1, 2)), -0.2, 0.2)), 0.005, 2.0)
    d_skip = jnp.clip(0.5 + 1.0 * jax.random.uniform(splits[11], (G, HG), jnp.float32) ** shard_levels(splits[11], (G, HG), ((0, 4), (1, 2)), -0.2, 0.2), 0.5, 1.5)
    norm_gain = jnp.clip(1.0 + 0.1 * jax.random.normal(splits[12], (G, HG * P_SIZE), jnp.float32), 0.5, 1.5)
    starts = draw_starts(jax.random.fold_in(splits[17], 71), 0)
    init_states = noise(splits[14], (SLOTS_ALL, G, HG, P_SIZE, N), 0.2, 1.2, ((0, 32), (1, 4), (2, 2)), jnp.float32)
    conv_x_edges = noise(splits[15], (SLOTS_ALL, KCONV - 1, G, HG * P_SIZE), 1.0, 6.0, ((0, 32), (2, 4), (3, 2)))
    conv_bc_edges = noise(splits[16], (SLOTS_ALL, KCONV - 1, G, 2 * N), 1.0, 6.0, ((0, 32), (2, 4)))
    return {"hidden": hidden, "w_x": w_x, "w_z": w_z, "w_bc": w_bc, "w_dt": w_dt, "conv_x_w": conv_x_w, "conv_bc_w": conv_bc_w, "conv_x_bias": conv_x_bias, "conv_bc_bias": conv_bc_bias, "dt_bias": dt_bias, "decay_rate": decay_rate, "d_skip": d_skip, "norm_gain": norm_gain, "starts": starts, "init_states": init_states, "conv_x_edges": conv_x_edges, "conv_bc_edges": conv_bc_edges}


PRECISE = lax.Precision.HIGHEST
EPSILON = 1e-05

def local_terms(x_vals, b_proj, c_proj, dt_vals, flag_vals, init_vals, rate_vals):
    rows_here = x_vals.shape[0]
    slot_total = init_vals.shape[0]
    positions = jnp.arange(rows_here, dtype=jnp.int32)
    segment = jnp.cumsum(flag_vals.astype(jnp.int32)).astype(jnp.int32)
    started = segment[rows_here - 1]
    log_decay = -dt_vals * rate_vals[None, :]
    cumulative = jnp.cumsum(log_decay, axis=0)
    preceding = cumulative - log_decay
    start_at = lax.cummax(jnp.where(flag_vals, positions, 0), axis=0)
    baseline = jnp.where((segment > 0)[:, None], preceding[start_at], 0.0)
    joined = (segment[:, None] == segment[None, :]) & (positions[:, None] >= positions[None, :])
    intersection = jnp.dot(c_proj, b_proj.T, preferred_element_type=jnp.float32)
    cumul_t = cumulative.T
    spread = jnp.where(joined[None], cumul_t[:, :, None] - cumul_t[:, None, :], 0.0)
    mixing = jnp.where(joined[None], jnp.exp(spread), 0.0) * intersection[None] * dt_vals.T[:, None, :]
    internal = jnp.einsum('hij,jhp->ihp', mixing, x_vals.astype(jnp.float32), precision=PRECISE)
    from_slot = jnp.einsum('tn,shpn->tshp', c_proj.astype(jnp.float32), init_vals, precision=PRECISE)
    slot_ids = jnp.arange(1, slot_total + 1, dtype=jnp.int32)
    chosen = (segment[:, None] == slot_ids[None, :]).astype(jnp.float32)
    restarted = jnp.einsum('ts,tshp->thp', chosen, from_slot, precision=PRECISE)
    y_part = internal + jnp.exp(cumulative - baseline)[:, :, None] * restarted
    carried = jnp.where((segment == 0)[:, None], jnp.exp(cumulative), 0.0)
    indices = jnp.arange(slot_total + 1, dtype=jnp.int32)
    belongs = segment[:, None] == indices[None, :]
    last_at = lax.optimization_barrier(jnp.max(jnp.where(belongs, positions[:, None], -1), axis=0))
    first_at = lax.optimization_barrier(jnp.min(jnp.where(belongs, positions[:, None], rows_here), axis=0))
    cumul_end = jnp.where((last_at >= 0)[:, None], cumulative[jnp.maximum(last_at, 0)], 0.0)
    lag_spread = jnp.where(belongs.T[:, :, None], cumul_end[:, None, :] - cumulative[None], 0.0)
    weights = jnp.where(belongs.T[:, :, None], jnp.exp(lag_spread), 0.0) * dt_vals[None]
    weighted = weights[..., None] * x_vals.astype(jnp.float32)[None]
    gathered = jnp.einsum('sthp,tn->shpn', weighted, b_proj.astype(jnp.float32), precision=PRECISE)
    base_slot = preceding[jnp.minimum(first_at, rows_here - 1)]
    factor = jnp.exp(jnp.where((slot_ids <= started)[:, None], cumul_end[1:] - base_slot[1:], 0.0))
    in_use = slot_ids <= started
    seg_rest = gathered[1:] + jnp.where(in_use[:, None, None, None], factor[..., None, None] * init_vals, 0.0)
    seg_ends = jnp.concatenate([gathered[:1], seg_rest], axis=0)
    decay_all = jnp.where(started == 0, jnp.exp(cumulative[rows_here - 1]), 0.0)
    state_add = lax.optimization_barrier(jnp.sum(jnp.where((indices == started)[:, None, None, None], seg_ends, 0.0), axis=0))
    return (y_part, carried, seg_ends, decay_all, state_add, cumul_end[0], started)

def convolve(raw, edges, kernel, offset_bias, start_at, slot_of, positions):
    lagged = KCONV - 1
    total = offset_bias[None].astype(jnp.float32) + kernel[lagged][None].astype(jnp.float32) * raw.astype(jnp.float32)
    for offset in range(1, lagged + 1):
        source = positions - offset
        inside = source >= start_at
        row_pick = jnp.clip(lagged - start_at + source, 0, lagged - 1)
        earlier = raw[jnp.maximum(source, 0)]
        from_edge = edges[slot_of, row_pick]
        chosen = jnp.where(inside[:, None, None], earlier, from_edge).astype(jnp.float32)
        total = total + kernel[lagged - offset][None].astype(jnp.float32) * chosen
    return jax.nn.silu(total).astype(jnp.bfloat16)

def reference(hidden, w_x, w_z, w_bc, w_dt, conv_x_w, conv_bc_w, conv_x_bias, conv_bc_bias, dt_bias, decay_rate, d_skip, norm_gain, starts, init_states, conv_x_edges, conv_bc_edges):

    def project(weight):
        columns = weight.shape[1] * weight.shape[2]
        result = jnp.dot(hidden, weight.reshape(D, columns), preferred_element_type=jnp.float32)
        return result.reshape(TOKENS, weight.shape[1], weight.shape[2]).astype(jnp.bfloat16)
    x_raw = project(w_x)
    z_gate = project(w_z)
    bc_raw = project(w_bc)
    dt_raw = project(w_dt)
    positions = jnp.arange(TOKENS, dtype=jnp.int32)
    flag_vals = starts == 1
    start_at = lax.cummax(jnp.where(flag_vals, positions, 0), axis=0)
    local_cum = jnp.cumsum(starts.reshape(N_SEQ, TOK_DEV), axis=1).astype(jnp.int32).reshape(TOKENS)
    slot_of = (start_at // TOK_DEV * SLOTS + local_cum[start_at] - 1).astype(jnp.int32)
    x_conv = convolve(x_raw, conv_x_edges, conv_x_w, conv_x_bias, start_at, slot_of, positions)
    bc_conv = convolve(bc_raw, conv_bc_edges, conv_bc_w, conv_bc_bias, start_at, slot_of, positions)
    dt_vals = jax.nn.softplus(dt_raw.astype(jnp.float32) + dt_bias[None])
    x_blocks = x_conv.reshape(N_SEQ, TOK_DEV, G, HG, P_SIZE)
    b_blocks = bc_conv[..., :N].reshape(N_SEQ, TOK_DEV, G, N)
    c_blocks = bc_conv[..., N:].reshape(N_SEQ, TOK_DEV, G, N)
    dt_blocks = dt_vals.reshape(N_SEQ, TOK_DEV, G, HG)
    flag_blocks = flag_vals.reshape(N_SEQ, TOK_DEV)
    init_blocks = init_states.reshape(N_SEQ, SLOTS, G, HG, P_SIZE, N)
    group_terms = jax.vmap(local_terms, in_axes=(1, 1, 1, 1, None, 1, 0), out_axes=0)

    def advance(carry, block):
        x_b, b_b, c_b, dt_b, flag_b, init_b = block
        y_part, carried, seg_ends, decay_all, state_add, end_zero, started = group_terms(x_b, b_b, c_b, dt_b, flag_b, init_b, decay_rate)
        carried_in = jnp.einsum('tgn,ghpn->gthp', c_b.astype(jnp.float32), carry, precision=PRECISE)
        y_block = y_part + carried[..., None] * carried_in
        entering = seg_ends[:, 0] + jnp.exp(end_zero)[..., None, None] * carry
        new_carry = decay_all[..., None, None] * carry + state_add
        return (new_carry, (y_block, entering, seg_ends, started[0]))
    zero_state = jnp.zeros((G, HG, P_SIZE, N), jnp.float32)
    _, (y_all, entering_all, ends_all, counts) = lax.scan(advance, zero_state, (x_blocks, b_blocks, c_blocks, dt_blocks, flag_blocks, init_blocks))
    y_tokens = jnp.transpose(y_all, (0, 2, 1, 3, 4)) + d_skip[None, None, :, :, None] * x_blocks.astype(jnp.float32)
    y_flat = y_tokens.reshape(TOKENS, G, HG * P_SIZE)
    block_ids = jnp.arange(N_SEQ, dtype=jnp.int32)
    marked = jnp.where(counts > 0, block_ids, N_SEQ).astype(jnp.int32)
    following = lax.cummin(marked, axis=0, reverse=True)
    next_block = jnp.concatenate([following[1:], jnp.full((1,), N_SEQ, jnp.int32)])
    found = next_block < N_SEQ
    from_right = entering_all[jnp.minimum(next_block, N_SEQ - 1)]
    pieces = []
    for slot in range(1, SLOTS + 1):
        own = ends_all[:, :, slot]
        tail_state = jnp.where(found[:, None, None, None, None], from_right, own)
        picked = jnp.where((counts == slot)[:, None, None, None, None], tail_state, jnp.where((counts > slot)[:, None, None, None, None], own, 0.0))
        pieces.append(picked)
    final_states = jnp.stack(pieces, axis=1).reshape(SLOTS_ALL, G, HG, P_SIZE, N)
    gated = y_flat * jax.nn.silu(z_gate.astype(jnp.float32))
    mean_sq = lax.optimization_barrier(jnp.mean(gated * gated, axis=-1, keepdims=True))
    gated_out = (gated * lax.rsqrt(mean_sq + EPSILON) * norm_gain[None]).astype(jnp.bfloat16)
    return (gated_out, final_states)
```

```python
import jax
import jax.numpy as jnp
from jax import lax
from jax.sharding import PartitionSpec as P

P_SIZE = 64
N = 128


PRECISE = lax.Precision.HIGHEST
EPSILON = 1e-05


def from_behind(value, axis, steps):
    count = lax.axis_size(axis)
    first, last = (max(0, -steps), min(count, count - steps))
    return lax.ppermute(value, axis, [(source, source + steps) for source in range(first, last)])


def local_terms(x_vals, b_proj, c_proj, dt_vals, flag_vals, init_vals, rate_vals):
    rows_here = x_vals.shape[0]
    slot_total = init_vals.shape[0]
    positions = jnp.arange(rows_here, dtype=jnp.int32)
    segment = jnp.cumsum(flag_vals.astype(jnp.int32))
    started = segment[rows_here - 1]
    log_decay = -dt_vals * rate_vals[None, :]
    cumulative = jnp.cumsum(log_decay, axis=0)
    preceding = cumulative - log_decay
    start_at = lax.cummax(jnp.where(flag_vals, positions, 0), axis=0)
    baseline = jnp.where((segment > 0)[:, None], preceding[start_at], 0.0)
    joined = (segment[:, None] == segment[None, :]) & (positions[:, None] >= positions[None, :])
    intersection = jnp.dot(c_proj, b_proj.T, preferred_element_type=jnp.float32)
    cumul_t = cumulative.T
    spread = jnp.where(joined[None], cumul_t[:, :, None] - cumul_t[:, None, :], 0.0)
    mixing = (
        jnp.where(joined[None], jnp.exp(spread), 0.0) * intersection[None] * dt_vals.T[:, None, :]
    )
    internal = jnp.einsum("hij,jhp->ihp", mixing, x_vals.astype(jnp.float32), precision=PRECISE)
    from_slot = jnp.einsum(
        "tn,shpn->tshp", c_proj.astype(jnp.float32), init_vals, precision=PRECISE
    )
    slot_ids = jnp.arange(1, slot_total + 1, dtype=jnp.int32)
    chosen = (segment[:, None] == slot_ids[None, :]).astype(jnp.float32)
    restarted = jnp.einsum("ts,tshp->thp", chosen, from_slot, precision=PRECISE)
    y_part = internal + jnp.exp(cumulative - baseline)[:, :, None] * restarted
    carried = jnp.where((segment == 0)[:, None], jnp.exp(cumulative), 0.0)
    indices = jnp.arange(slot_total + 1, dtype=jnp.int32)
    belongs = segment[:, None] == indices[None, :]
    last_at = jnp.max(jnp.where(belongs, positions[:, None], -1), axis=0)
    first_at = jnp.min(jnp.where(belongs, positions[:, None], rows_here), axis=0)
    cumul_end = jnp.where((last_at >= 0)[:, None], cumulative[jnp.maximum(last_at, 0)], 0.0)
    lag_spread = jnp.where(belongs.T[:, :, None], cumul_end[:, None, :] - cumulative[None], 0.0)
    weights = jnp.where(belongs.T[:, :, None], jnp.exp(lag_spread), 0.0) * dt_vals[None]
    weighted = weights[..., None] * x_vals.astype(jnp.float32)[None]
    gathered = jnp.einsum("sthp,tn->shpn", weighted, b_proj.astype(jnp.float32), precision=PRECISE)
    base_slot = preceding[jnp.minimum(first_at, rows_here - 1)]
    factor = jnp.exp(jnp.where((slot_ids <= started)[:, None], cumul_end[1:] - base_slot[1:], 0.0))
    in_use = slot_ids <= started
    seg_rest = gathered[1:] + jnp.where(
        in_use[:, None, None, None], factor[..., None, None] * init_vals, 0.0
    )
    seg_ends = jnp.concatenate([gathered[:1], seg_rest], axis=0)
    decay_all = jnp.where(started == 0, jnp.exp(cumulative[rows_here - 1]), 0.0)
    state_add = jnp.sum(jnp.where((indices == started)[:, None, None, None], seg_ends, 0.0), axis=0)
    return (y_part, carried, seg_ends, decay_all, state_add, cumul_end[0], started)


def tail_rows(raw, edges, start_last, segment_last, lagged):
    rows_here = raw.shape[0]
    source = jnp.arange(rows_here - lagged, rows_here, dtype=jnp.int32)
    inside = source >= start_last
    row_pick = jnp.clip(lagged - start_last + source, 0, lagged - 1)
    from_edge = edges[jnp.maximum(segment_last - 1, 0), row_pick]
    return jnp.where(inside[:, None], raw[rows_here - lagged :], from_edge)


def convolve(raw, prior, edges, kernel, offset_bias, start_at, segment, positions, lagged):
    rows_here = raw.shape[0]
    slot_total = edges.shape[0]
    extended = jnp.concatenate([prior, raw], axis=0)
    table = edges.reshape(slot_total * lagged, edges.shape[-1])
    total = offset_bias[None].astype(jnp.float32) + kernel[lagged][None].astype(
        jnp.float32
    ) * raw.astype(jnp.float32)
    for offset in range(1, lagged + 1):
        source = positions - offset
        inside = source >= start_at
        row_pick = jnp.clip(lagged - start_at + source, 0, lagged - 1)
        which = jnp.maximum(segment - 1, 0) * lagged + row_pick
        picker = (
            which[:, None] == jnp.arange(slot_total * lagged, dtype=jnp.int32)[None, :]
        ).astype(jnp.bfloat16)
        from_edge = jnp.dot(picker, table, preferred_element_type=jnp.float32)
        earlier = extended[lagged - offset : lagged - offset + rows_here].astype(jnp.float32)
        total = total + kernel[lagged - offset][None].astype(jnp.float32) * jnp.where(
            inside[:, None], earlier, from_edge
        )
    return jax.nn.silu(total).astype(jnp.bfloat16)


def shards(
    hidden,
    w_x,
    w_z,
    w_bc,
    w_dt,
    conv_x_w,
    conv_bc_w,
    conv_x_bias,
    conv_bc_bias,
    dt_bias,
    decay_rate,
    d_skip,
    norm_gain,
    starts,
    init_states,
    conv_x_edges,
    conv_bc_edges,
):
    tokens = lax.all_gather(hidden, "row", axis=0, tiled=True)
    rows_here = tokens.shape[0]
    channels = w_x.shape[2]
    heads_here = w_dt.shape[2]
    lagged = conv_x_w.shape[0] - 1
    pieces = [
        jnp.einsum("td,dgc->gtc", tokens, weight, preferred_element_type=jnp.float32)
        for weight in (w_x, w_z, w_bc, w_dt)
    ]
    summed = lax.psum_scatter(
        jnp.concatenate(pieces, axis=2), "col", scatter_dimension=0, tiled=True
    )
    mixed = summed[0].astype(jnp.bfloat16)
    x_raw = mixed[:, :channels]
    z_gate = mixed[:, channels : 2 * channels]
    bc_raw = mixed[:, 2 * channels : 2 * channels + 2 * N]
    dt_raw = mixed[:, 2 * channels + 2 * N :]
    positions = jnp.arange(rows_here, dtype=jnp.int32)
    flag_vals = starts == 1
    segment = jnp.cumsum(starts)
    start_at = lax.cummax(jnp.where(flag_vals, positions, -lagged), axis=0)
    x_edges = conv_x_edges[:, :, 0]
    bc_edges = conv_bc_edges[:, :, 0]
    start_last = start_at[rows_here - 1]
    segment_last = segment[rows_here - 1]
    send_x = tail_rows(x_raw, x_edges, start_last, segment_last, lagged)
    send_bc = tail_rows(bc_raw, bc_edges, start_last, segment_last, lagged)
    prior_x, prior_bc = from_behind((send_x, send_bc), "seq", 1)
    x_conv = convolve(
        x_raw,
        prior_x,
        x_edges,
        conv_x_w[:, 0],
        conv_x_bias[0],
        start_at,
        segment,
        positions,
        lagged,
    )
    bc_conv = convolve(
        bc_raw,
        prior_bc,
        bc_edges,
        conv_bc_w[:, 0],
        conv_bc_bias[0],
        start_at,
        segment,
        positions,
        lagged,
    )
    x_heads = x_conv.reshape(rows_here, heads_here, P_SIZE)
    b_proj = bc_conv[:, :N]
    c_proj = bc_conv[:, N:]
    dt_vals = jax.nn.softplus(dt_raw.astype(jnp.float32) + dt_bias[0][None, :])
    init_vals = init_states[:, 0]
    y_part, carried, seg_ends, decay_all, state_add, end_zero, started = local_terms(
        x_heads, b_proj, c_proj, dt_vals, flag_vals, init_vals, decay_rate[0]
    )

    seq_count = lax.axis_size("seq")
    seq_at = lax.axis_index("seq")
    heads_n, p_n, n_n = state_add.shape
    ones = jnp.ones((heads_n,), jnp.float32)
    zeros_state = jnp.zeros_like(state_add)
    has_start = jnp.where(started > 0, 1.0, 0.0).astype(jnp.float32)

    def pack(decay, state, mark):
        aux = jnp.concatenate(
            [
                jnp.broadcast_to(decay[:, None], (heads_n, n_n // 2)),
                jnp.broadcast_to(mark, (heads_n, n_n - n_n // 2)),
            ],
            axis=1,
        )
        return jnp.concatenate([state, aux[:, None, :]], axis=1)

    def unpack(packed):
        return packed[:, p_n, 0], packed[:, :p_n], packed[0, p_n, n_n - 1]

    fwd_in = (decay_all * ones, state_add)
    fwd_ex = (ones, zeros_state)
    bwd_in = (jnp.exp(end_zero), seg_ends[0], has_start)
    bwd_ex = (ones, zeros_state, jnp.zeros((), jnp.float32))
    shift = 1
    while shift < seq_count:
        last = 2 * shift >= seq_count
        got_f = from_behind(pack(fwd_in[0], fwd_in[1], 0.0), "seq", shift)
        got_b = from_behind(pack(*bwd_in), "seq", -shift)
        early_a, early_b, _ = unpack(got_f)
        late_a, late_b, late_m = unpack(got_b)
        late_ok = seq_at + shift < seq_count
        fwd_ex = (
            fwd_ex[0] * early_a,
            fwd_ex[0][:, None, None] * early_b + fwd_ex[1],
        )

        def near_far(near, far_a, far_b, far_m):
            keep = (near[2] > 0.5) | jnp.logical_not(late_ok)
            return (
                jnp.where(keep, near[0], far_a * near[0]),
                jnp.where(keep, near[1], far_a[:, None, None] * near[1] + far_b),
                jnp.where(keep, near[2], far_m),
            )

        bwd_ex = near_far(bwd_ex, late_a, late_b, late_m)
        if not last:
            fwd_in = (
                fwd_in[0] * early_a,
                fwd_in[0][:, None, None] * early_b + fwd_in[1],
            )
            bwd_in = near_far(bwd_in, late_a, late_b, late_m)
        shift *= 2
    state_in = fwd_ex[1]
    carried_in = jnp.einsum("tn,hpn->thp", c_proj.astype(jnp.float32), state_in, precision=PRECISE)
    y_full = (
        y_part
        + carried[:, :, None] * carried_in
        + d_skip[0][None, :, None] * x_heads.astype(jnp.float32)
    )
    tail_state = bwd_ex[0][:, None, None] * state_add + bwd_ex[1]
    slot_ids = jnp.arange(1, init_vals.shape[0] + 1, dtype=jnp.int32)
    finals = jnp.where(
        (slot_ids < started)[:, None, None, None],
        seg_ends[1:],
        jnp.where((slot_ids == started)[:, None, None, None], tail_state[None], 0.0),
    )
    gated = y_full.reshape(rows_here, channels) * jax.nn.silu(z_gate.astype(jnp.float32))
    partial_sq = jnp.sum(gated * gated, axis=-1)
    total_sq = lax.psum(partial_sq, "row")
    mean_sq = total_sq / (channels * lax.axis_size("row"))
    gated_out = (gated * lax.rsqrt(mean_sq + EPSILON)[:, None] * norm_gain[0][None, :]).astype(
        jnp.bfloat16
    )
    return (gated_out.reshape(rows_here, 1, channels), finals[:, None])


def solution(mesh):
    placed = (
        P(("seq", "row"), "col"),
        P("col", None, "row"),
        P("col", None, "row"),
        P("col", None, None),
        P("col", None, "row"),
        P(None, "col", "row"),
        P(None, "col", None),
        P("col", "row"),
        P("col", None),
        P("col", "row"),
        P("col", "row"),
        P("col", "row"),
        P("col", "row"),
        P("seq"),
        P("seq", "col", "row", None, None),
        P("seq", None, "col", "row"),
        P("seq", None, "col", None),
    )
    return jax.shard_map(
        shards,
        mesh=mesh,
        in_specs=placed,
        out_specs=(P("seq", "col", "row"), P("seq", "col", "row", None, None)),
        check_vma=False,
    )
```

```python
import jax
import jax.numpy as jnp
from jax import lax
from jax.sharding import PartitionSpec as P

P_SIZE = 64
N = 128


PRECISE = lax.Precision.HIGHEST
EPSILON = 1e-05


def from_behind(value, axis, steps):
    count = lax.axis_size(axis)
    first, last = (max(0, -steps), min(count, count - steps))
    return lax.ppermute(value, axis, [(source, source + steps) for source in range(first, last)])


def local_terms(x_vals, b_proj, c_proj, dt_vals, flag_vals, init_vals, rate_vals):
    rows_here = x_vals.shape[0]
    slot_total = init_vals.shape[0]
    positions = jnp.arange(rows_here, dtype=jnp.int32)
    segment = jnp.cumsum(flag_vals.astype(jnp.int32))
    started = segment[rows_here - 1]
    log_decay = -dt_vals * rate_vals[None, :]
    cumulative = jnp.cumsum(log_decay, axis=0)
    preceding = cumulative - log_decay
    start_at = lax.cummax(jnp.where(flag_vals, positions, 0), axis=0)
    baseline = jnp.where((segment > 0)[:, None], preceding[start_at], 0.0)
    joined = (segment[:, None] == segment[None, :]) & (positions[:, None] >= positions[None, :])
    intersection = jnp.dot(c_proj, b_proj.T, preferred_element_type=jnp.float32)
    cumul_t = cumulative.T
    spread = jnp.where(joined[None], cumul_t[:, :, None] - cumul_t[:, None, :], 0.0)
    mixing = (
        jnp.where(joined[None], jnp.exp(spread), 0.0) * intersection[None] * dt_vals.T[:, None, :]
    )
    internal = jnp.einsum("hij,jhp->ihp", mixing, x_vals.astype(jnp.float32), precision=PRECISE)
    from_slot = jnp.einsum(
        "tn,shpn->tshp", c_proj.astype(jnp.float32), init_vals, precision=PRECISE
    )
    slot_ids = jnp.arange(1, slot_total + 1, dtype=jnp.int32)
    chosen = (segment[:, None] == slot_ids[None, :]).astype(jnp.float32)
    restarted = jnp.einsum("ts,tshp->thp", chosen, from_slot, precision=PRECISE)
    y_part = internal + jnp.exp(cumulative - baseline)[:, :, None] * restarted
    carried = jnp.where((segment == 0)[:, None], jnp.exp(cumulative), 0.0)
    indices = jnp.arange(slot_total + 1, dtype=jnp.int32)
    belongs = segment[:, None] == indices[None, :]
    last_at = jnp.max(jnp.where(belongs, positions[:, None], -1), axis=0)
    first_at = jnp.min(jnp.where(belongs, positions[:, None], rows_here), axis=0)
    cumul_end = jnp.where((last_at >= 0)[:, None], cumulative[jnp.maximum(last_at, 0)], 0.0)
    lag_spread = jnp.where(belongs.T[:, :, None], cumul_end[:, None, :] - cumulative[None], 0.0)
    weights = jnp.where(belongs.T[:, :, None], jnp.exp(lag_spread), 0.0) * dt_vals[None]
    weighted = weights[..., None] * x_vals.astype(jnp.float32)[None]
    gathered = jnp.einsum("sthp,tn->shpn", weighted, b_proj.astype(jnp.float32), precision=PRECISE)
    base_slot = preceding[jnp.minimum(first_at, rows_here - 1)]
    factor = jnp.exp(jnp.where((slot_ids <= started)[:, None], cumul_end[1:] - base_slot[1:], 0.0))
    in_use = slot_ids <= started
    seg_rest = gathered[1:] + jnp.where(
        in_use[:, None, None, None], factor[..., None, None] * init_vals, 0.0
    )
    seg_ends = jnp.concatenate([gathered[:1], seg_rest], axis=0)
    decay_all = jnp.where(started == 0, jnp.exp(cumulative[rows_here - 1]), 0.0)
    state_add = jnp.sum(jnp.where((indices == started)[:, None, None, None], seg_ends, 0.0), axis=0)
    return (y_part, carried, seg_ends, decay_all, state_add, cumul_end[0], started)


def tail_rows(raw, edges, start_last, segment_last, lagged):
    rows_here = raw.shape[0]
    source = jnp.arange(rows_here - lagged, rows_here, dtype=jnp.int32)
    inside = source >= start_last
    row_pick = jnp.clip(lagged - start_last + source, 0, lagged - 1)
    from_edge = edges[jnp.maximum(segment_last - 1, 0), row_pick]
    return jnp.where(inside[:, None], raw[rows_here - lagged :], from_edge)


def convolve(raw, prior, edges, kernel, offset_bias, start_at, segment, positions, lagged):
    rows_here = raw.shape[0]
    slot_total = edges.shape[0]
    extended = jnp.concatenate([prior, raw], axis=0)
    table = edges.reshape(slot_total * lagged, edges.shape[-1])
    total = offset_bias[None].astype(jnp.float32) + kernel[lagged][None].astype(
        jnp.float32
    ) * raw.astype(jnp.float32)
    for offset in range(1, lagged + 1):
        source = positions - offset
        inside = source >= start_at
        row_pick = jnp.clip(lagged - start_at + source, 0, lagged - 1)
        which = jnp.maximum(segment - 1, 0) * lagged + row_pick
        picker = (
            which[:, None] == jnp.arange(slot_total * lagged, dtype=jnp.int32)[None, :]
        ).astype(jnp.bfloat16)
        from_edge = jnp.dot(picker, table, preferred_element_type=jnp.float32)
        earlier = extended[lagged - offset : lagged - offset + rows_here].astype(jnp.float32)
        total = total + kernel[lagged - offset][None].astype(jnp.float32) * jnp.where(
            inside[:, None], earlier, from_edge
        )
    return jax.nn.silu(total).astype(jnp.bfloat16)


def shards(
    hidden,
    w_x,
    w_z,
    w_bc,
    w_dt,
    conv_x_w,
    conv_bc_w,
    conv_x_bias,
    conv_bc_bias,
    dt_bias,
    decay_rate,
    d_skip,
    norm_gain,
    starts,
    init_states,
    conv_x_edges,
    conv_bc_edges,
):
    tokens = lax.all_gather(hidden, "row", axis=0, tiled=True)
    rows_here = tokens.shape[0]
    channels = w_x.shape[2]
    heads_here = w_dt.shape[2]
    lagged = conv_x_w.shape[0] - 1
    pieces = [
        jnp.einsum("td,dgc->gtc", tokens, weight, preferred_element_type=jnp.float32)
        for weight in (w_x, w_z, w_bc, w_dt)
    ]
    summed = lax.psum_scatter(
        jnp.concatenate(pieces, axis=2), "col", scatter_dimension=0, tiled=True
    )
    mixed = summed[0].astype(jnp.bfloat16)
    x_raw = mixed[:, :channels]
    z_gate = mixed[:, channels : 2 * channels]
    bc_raw = mixed[:, 2 * channels : 2 * channels + 2 * N]
    dt_raw = mixed[:, 2 * channels + 2 * N :]
    positions = jnp.arange(rows_here, dtype=jnp.int32)
    flag_vals = starts == 1
    segment = jnp.cumsum(starts)
    start_at = lax.cummax(jnp.where(flag_vals, positions, -lagged), axis=0)
    x_edges = conv_x_edges[:, :, 0]
    bc_edges = conv_bc_edges[:, :, 0]
    start_last = start_at[rows_here - 1]
    segment_last = segment[rows_here - 1]
    send_x = tail_rows(x_raw, x_edges, start_last, segment_last, lagged)
    send_bc = tail_rows(bc_raw, bc_edges, start_last, segment_last, lagged)
    prior_x, prior_bc = from_behind((send_x, send_bc), "seq", 1)
    x_conv = convolve(
        x_raw,
        prior_x,
        x_edges,
        conv_x_w[:, 0],
        conv_x_bias[0],
        start_at,
        segment,
        positions,
        lagged,
    )
    bc_conv = convolve(
        bc_raw,
        prior_bc,
        bc_edges,
        conv_bc_w[:, 0],
        conv_bc_bias[0],
        start_at,
        segment,
        positions,
        lagged,
    )
    x_heads = x_conv.reshape(rows_here, heads_here, P_SIZE)
    b_proj = bc_conv[:, :N]
    c_proj = bc_conv[:, N:]
    dt_vals = jax.nn.softplus(dt_raw.astype(jnp.float32) + dt_bias[0][None, :])
    init_vals = init_states[:, 0]
    y_part, carried, seg_ends, decay_all, state_add, end_zero, started = local_terms(
        x_heads, b_proj, c_proj, dt_vals, flag_vals, init_vals, decay_rate[0]
    )

    seq_count = lax.axis_size("seq")
    seq_at = lax.axis_index("seq")
    heads_n, p_n, n_n = state_add.shape
    ones = jnp.ones((heads_n,), jnp.float32)
    zeros_state = jnp.zeros_like(state_add)
    has_start = jnp.where(started > 0, 1.0, 0.0).astype(jnp.float32)

    def pack(decay, state, mark):
        aux = jnp.concatenate(
            [
                jnp.broadcast_to(decay[:, None], (heads_n, n_n // 2)),
                jnp.broadcast_to(mark, (heads_n, n_n - n_n // 2)),
            ],
            axis=1,
        )
        return jnp.concatenate([state, aux[:, None, :]], axis=1)

    def unpack(packed):
        return packed[:, p_n, 0], packed[:, :p_n], packed[0, p_n, n_n - 1]

    fwd_in = (decay_all * ones, state_add)
    fwd_ex = (ones, zeros_state)
    bwd_in = (jnp.exp(end_zero), seg_ends[0], has_start)
    bwd_ex = (ones, zeros_state, jnp.zeros((), jnp.float32))
    shift = 1
    while shift < seq_count:
        last = 2 * shift >= seq_count
        got_f = from_behind(pack(fwd_in[0], fwd_in[1], 0.0), "seq", shift)
        got_b = from_behind(pack(*bwd_in), "seq", -shift)
        early_a, early_b, _ = unpack(got_f)
        late_a, late_b, late_m = unpack(got_b)
        late_ok = seq_at + shift < seq_count
        fwd_ex = (
            fwd_ex[0] * early_a,
            fwd_ex[0][:, None, None] * early_b + fwd_ex[1],
        )

        def near_far(near, far_a, far_b, far_m):
            keep = (near[2] > 0.5) | jnp.logical_not(late_ok)
            return (
                jnp.where(keep, near[0], far_a * near[0]),
                jnp.where(keep, near[1], far_a[:, None, None] * near[1] + far_b),
                jnp.where(keep, near[2], far_m),
            )

        bwd_ex = near_far(bwd_ex, late_a, late_b, late_m)
        if not last:
            fwd_in = (
                fwd_in[0] * early_a,
                fwd_in[0][:, None, None] * early_b + fwd_in[1],
            )
            bwd_in = near_far(bwd_in, late_a, late_b, late_m)
        fwd_in, fwd_ex, bwd_in, bwd_ex = lax.optimization_barrier((fwd_in, fwd_ex, bwd_in, bwd_ex))
        shift *= 2
    state_in = fwd_ex[1]
    carried_in = jnp.einsum("tn,hpn->thp", c_proj.astype(jnp.float32), state_in, precision=PRECISE)
    y_full = (
        y_part
        + carried[:, :, None] * carried_in
        + d_skip[0][None, :, None] * x_heads.astype(jnp.float32)
    )
    tail_state = bwd_ex[0][:, None, None] * state_add + bwd_ex[1]
    slot_ids = jnp.arange(1, init_vals.shape[0] + 1, dtype=jnp.int32)
    finals = jnp.where(
        (slot_ids < started)[:, None, None, None],
        seg_ends[1:],
        jnp.where((slot_ids == started)[:, None, None, None], tail_state[None], 0.0),
    )
    gated = y_full.reshape(rows_here, channels) * jax.nn.silu(z_gate.astype(jnp.float32))
    partial_sq = jnp.sum(gated * gated, axis=-1)
    total_sq = lax.psum(partial_sq, "row")
    mean_sq = total_sq / (channels * lax.axis_size("row"))
    gated_out = (gated * lax.rsqrt(mean_sq + EPSILON)[:, None] * norm_gain[0][None, :]).astype(
        jnp.bfloat16
    )
    return (gated_out.reshape(rows_here, 1, channels), finals[:, None])


def solution(mesh):
    placed = (
        P(("seq", "row"), "col"),
        P("col", None, "row"),
        P("col", None, "row"),
        P("col", None, None),
        P("col", None, "row"),
        P(None, "col", "row"),
        P(None, "col", None),
        P("col", "row"),
        P("col", None),
        P("col", "row"),
        P("col", "row"),
        P("col", "row"),
        P("col", "row"),
        P("seq"),
        P("seq", "col", "row", None, None),
        P("seq", None, "col", "row"),
        P("seq", None, "col", None),
    )
    return jax.shard_map(
        shards,
        mesh=mesh,
        in_specs=placed,
        out_specs=(P("seq", "col", "row"), P("seq", "col", "row", None, None)),
        check_vma=False,
    )
```

```python
import jax
import jax.numpy as jnp
from jax import lax
from jax.sharding import PartitionSpec as P

P_SIZE = 64
N = 128


PRECISE = lax.Precision.HIGHEST
EPSILON = 1e-05


def from_behind(value, axis, steps):
    count = lax.axis_size(axis)
    first, last = (max(0, -steps), min(count, count - steps))
    return lax.ppermute(value, axis, [(source, source + steps) for source in range(first, last)])


def local_terms(x_vals, b_proj, c_proj, dt_vals, flag_vals, init_vals, rate_vals):
    rows_here = x_vals.shape[0]
    slot_total = init_vals.shape[0]
    positions = jnp.arange(rows_here, dtype=jnp.int32)
    segment = jnp.cumsum(flag_vals.astype(jnp.int32))
    started = segment[rows_here - 1]
    log_decay = -dt_vals * rate_vals[None, :]
    cumulative = jnp.cumsum(log_decay, axis=0)
    preceding = cumulative - log_decay
    start_at = lax.cummax(jnp.where(flag_vals, positions, 0), axis=0)
    baseline = jnp.where((segment > 0)[:, None], preceding[start_at], 0.0)
    joined = (segment[:, None] == segment[None, :]) & (positions[:, None] >= positions[None, :])
    intersection = jnp.dot(c_proj, b_proj.T, preferred_element_type=jnp.float32)
    cumul_t = cumulative.T
    spread = jnp.where(joined[None], cumul_t[:, :, None] - cumul_t[:, None, :], 0.0)
    mixing = (
        jnp.where(joined[None], jnp.exp(spread), 0.0) * intersection[None] * dt_vals.T[:, None, :]
    )
    internal = jnp.einsum("hij,jhp->ihp", mixing, x_vals.astype(jnp.float32), precision=PRECISE)
    from_slot = jnp.einsum(
        "tn,shpn->tshp", c_proj.astype(jnp.float32), init_vals, precision=PRECISE
    )
    slot_ids = jnp.arange(1, slot_total + 1, dtype=jnp.int32)
    chosen = (segment[:, None] == slot_ids[None, :]).astype(jnp.float32)
    restarted = jnp.einsum("ts,tshp->thp", chosen, from_slot, precision=PRECISE)
    y_part = internal + jnp.exp(cumulative - baseline)[:, :, None] * restarted
    carried = jnp.where((segment == 0)[:, None], jnp.exp(cumulative), 0.0)
    indices = jnp.arange(slot_total + 1, dtype=jnp.int32)
    belongs = segment[:, None] == indices[None, :]
    last_at = jnp.max(jnp.where(belongs, positions[:, None], -1), axis=0)
    first_at = jnp.min(jnp.where(belongs, positions[:, None], rows_here), axis=0)
    cumul_end = jnp.where((last_at >= 0)[:, None], cumulative[jnp.maximum(last_at, 0)], 0.0)
    lag_spread = jnp.where(belongs.T[:, :, None], cumul_end[:, None, :] - cumulative[None], 0.0)
    weights = jnp.where(belongs.T[:, :, None], jnp.exp(lag_spread), 0.0) * dt_vals[None]
    weighted = weights[..., None] * x_vals.astype(jnp.float32)[None]
    gathered = jnp.einsum("sthp,tn->shpn", weighted, b_proj.astype(jnp.float32), precision=PRECISE)
    base_slot = preceding[jnp.minimum(first_at, rows_here - 1)]
    factor = jnp.exp(jnp.where((slot_ids <= started)[:, None], cumul_end[1:] - base_slot[1:], 0.0))
    in_use = slot_ids <= started
    seg_rest = gathered[1:] + jnp.where(
        in_use[:, None, None, None], factor[..., None, None] * init_vals, 0.0
    )
    seg_ends = jnp.concatenate([gathered[:1], seg_rest], axis=0)
    decay_all = jnp.where(started == 0, jnp.exp(cumulative[rows_here - 1]), 0.0)
    state_add = jnp.sum(jnp.where((indices == started)[:, None, None, None], seg_ends, 0.0), axis=0)
    return (y_part, carried, seg_ends, decay_all, state_add, cumul_end[0], started)


def tail_rows(raw, edges, start_last, segment_last, lagged):
    rows_here = raw.shape[0]
    source = jnp.arange(rows_here - lagged, rows_here, dtype=jnp.int32)
    inside = source >= start_last
    row_pick = jnp.clip(lagged - start_last + source, 0, lagged - 1)
    from_edge = edges[jnp.maximum(segment_last - 1, 0), row_pick]
    return jnp.where(inside[:, None], raw[rows_here - lagged :], from_edge)


def convolve(raw, prior, edges, kernel, offset_bias, start_at, segment, positions, lagged):
    rows_here = raw.shape[0]
    slot_total = edges.shape[0]
    extended = jnp.concatenate([prior, raw], axis=0)
    table = edges.reshape(slot_total * lagged, edges.shape[-1])
    total = offset_bias[None].astype(jnp.float32) + kernel[lagged][None].astype(
        jnp.float32
    ) * raw.astype(jnp.float32)
    for offset in range(1, lagged + 1):
        source = positions - offset
        inside = source >= start_at
        row_pick = jnp.clip(lagged - start_at + source, 0, lagged - 1)
        which = jnp.maximum(segment - 1, 0) * lagged + row_pick
        picker = (
            which[:, None] == jnp.arange(slot_total * lagged, dtype=jnp.int32)[None, :]
        ).astype(jnp.bfloat16)
        from_edge = jnp.dot(picker, table, preferred_element_type=jnp.float32)
        earlier = extended[lagged - offset : lagged - offset + rows_here].astype(jnp.float32)
        total = total + kernel[lagged - offset][None].astype(jnp.float32) * jnp.where(
            inside[:, None], earlier, from_edge
        )
    return jax.nn.silu(total).astype(jnp.bfloat16)


def shards(
    hidden,
    w_x,
    w_z,
    w_bc,
    w_dt,
    conv_x_w,
    conv_bc_w,
    conv_x_bias,
    conv_bc_bias,
    dt_bias,
    decay_rate,
    d_skip,
    norm_gain,
    starts,
    init_states,
    conv_x_edges,
    conv_bc_edges,
):
    tokens = lax.all_gather(hidden, "row", axis=0, tiled=True)
    rows_here = tokens.shape[0]
    channels = w_x.shape[2]
    heads_here = w_dt.shape[2]
    lagged = conv_x_w.shape[0] - 1
    x_part, z_part, bc_part, dt_part = [
        jnp.einsum("td,dgc->gtc", tokens, weight, preferred_element_type=jnp.float32)
        for weight in (w_x, w_z, w_bc, w_dt)
    ]
    first = lax.psum_scatter(
        jnp.concatenate([x_part, bc_part, dt_part], axis=2), "col", scatter_dimension=0, tiled=True
    )[0].astype(jnp.bfloat16)
    first, z_part = lax.optimization_barrier((first, z_part))
    z_gate = lax.psum_scatter(z_part, "col", scatter_dimension=0, tiled=True)[0].astype(jnp.bfloat16)
    x_raw = first[:, :channels]
    bc_raw = first[:, channels : channels + 2 * N]
    dt_raw = first[:, channels + 2 * N :]
    positions = jnp.arange(rows_here, dtype=jnp.int32)
    flag_vals = starts == 1
    segment = jnp.cumsum(starts)
    start_at = lax.cummax(jnp.where(flag_vals, positions, -lagged), axis=0)
    x_edges = conv_x_edges[:, :, 0]
    bc_edges = conv_bc_edges[:, :, 0]
    start_last = start_at[rows_here - 1]
    segment_last = segment[rows_here - 1]
    send_x = tail_rows(x_raw, x_edges, start_last, segment_last, lagged)
    send_bc = tail_rows(bc_raw, bc_edges, start_last, segment_last, lagged)
    prior_x, prior_bc = from_behind((send_x, send_bc), "seq", 1)
    x_conv = convolve(
        x_raw,
        prior_x,
        x_edges,
        conv_x_w[:, 0],
        conv_x_bias[0],
        start_at,
        segment,
        positions,
        lagged,
    )
    bc_conv = convolve(
        bc_raw,
        prior_bc,
        bc_edges,
        conv_bc_w[:, 0],
        conv_bc_bias[0],
        start_at,
        segment,
        positions,
        lagged,
    )
    x_heads = x_conv.reshape(rows_here, heads_here, P_SIZE)
    b_proj = bc_conv[:, :N]
    c_proj = bc_conv[:, N:]
    dt_vals = jax.nn.softplus(dt_raw.astype(jnp.float32) + dt_bias[0][None, :])
    init_vals = init_states[:, 0]
    y_part, carried, seg_ends, decay_all, state_add, end_zero, started = local_terms(
        x_heads, b_proj, c_proj, dt_vals, flag_vals, init_vals, decay_rate[0]
    )

    seq_count = lax.axis_size("seq")
    seq_at = lax.axis_index("seq")
    heads_n, p_n, n_n = state_add.shape
    ones = jnp.ones((heads_n,), jnp.float32)
    zeros_state = jnp.zeros_like(state_add)
    has_start = jnp.where(started > 0, 1.0, 0.0).astype(jnp.float32)

    def pack(decay, state, mark):
        aux = jnp.concatenate(
            [
                jnp.broadcast_to(decay[:, None], (heads_n, n_n // 2)),
                jnp.broadcast_to(mark, (heads_n, n_n - n_n // 2)),
            ],
            axis=1,
        )
        return jnp.concatenate([state, aux[:, None, :]], axis=1)

    def unpack(packed):
        return packed[:, p_n, 0], packed[:, :p_n], packed[0, p_n, n_n - 1]

    fwd_in = (decay_all * ones, state_add)
    fwd_ex = (ones, zeros_state)
    bwd_in = (jnp.exp(end_zero), seg_ends[0], has_start)
    bwd_ex = (ones, zeros_state, jnp.zeros((), jnp.float32))
    shift = 1
    while shift < seq_count:
        last = 2 * shift >= seq_count
        got_f = from_behind(pack(fwd_in[0], fwd_in[1], 0.0), "seq", shift)
        got_b = from_behind(pack(*bwd_in), "seq", -shift)
        early_a, early_b, _ = unpack(got_f)
        late_a, late_b, late_m = unpack(got_b)
        late_ok = seq_at + shift < seq_count
        fwd_ex = (
            fwd_ex[0] * early_a,
            fwd_ex[0][:, None, None] * early_b + fwd_ex[1],
        )

        def near_far(near, far_a, far_b, far_m):
            keep = (near[2] > 0.5) | jnp.logical_not(late_ok)
            return (
                jnp.where(keep, near[0], far_a * near[0]),
                jnp.where(keep, near[1], far_a[:, None, None] * near[1] + far_b),
                jnp.where(keep, near[2], far_m),
            )

        bwd_ex = near_far(bwd_ex, late_a, late_b, late_m)
        if not last:
            fwd_in = (
                fwd_in[0] * early_a,
                fwd_in[0][:, None, None] * early_b + fwd_in[1],
            )
            bwd_in = near_far(bwd_in, late_a, late_b, late_m)
        fwd_in, fwd_ex, bwd_in, bwd_ex = lax.optimization_barrier((fwd_in, fwd_ex, bwd_in, bwd_ex))
        shift *= 2
    state_in = fwd_ex[1]
    carried_in = jnp.einsum("tn,hpn->thp", c_proj.astype(jnp.float32), state_in, precision=PRECISE)
    y_full = (
        y_part
        + carried[:, :, None] * carried_in
        + d_skip[0][None, :, None] * x_heads.astype(jnp.float32)
    )
    tail_state = bwd_ex[0][:, None, None] * state_add + bwd_ex[1]
    slot_ids = jnp.arange(1, init_vals.shape[0] + 1, dtype=jnp.int32)
    finals = jnp.where(
        (slot_ids < started)[:, None, None, None],
        seg_ends[1:],
        jnp.where((slot_ids == started)[:, None, None, None], tail_state[None], 0.0),
    )
    gated = y_full.reshape(rows_here, channels) * jax.nn.silu(z_gate.astype(jnp.float32))
    partial_sq = jnp.sum(gated * gated, axis=-1)
    total_sq = lax.psum(partial_sq, "row")
    mean_sq = total_sq / (channels * lax.axis_size("row"))
    gated_out = (gated * lax.rsqrt(mean_sq + EPSILON)[:, None] * norm_gain[0][None, :]).astype(
        jnp.bfloat16
    )
    return (gated_out.reshape(rows_here, 1, channels), finals[:, None])


def solution(mesh):
    placed = (
        P(("seq", "row"), "col"),
        P("col", None, "row"),
        P("col", None, "row"),
        P("col", None, None),
        P("col", None, "row"),
        P(None, "col", "row"),
        P(None, "col", None),
        P("col", "row"),
        P("col", None),
        P("col", "row"),
        P("col", "row"),
        P("col", "row"),
        P("col", "row"),
        P("seq"),
        P("seq", "col", "row", None, None),
        P("seq", None, "col", "row"),
        P("seq", None, "col", None),
    )
    return jax.shard_map(
        shards,
        mesh=mesh,
        in_specs=placed,
        out_specs=(P("seq", "col", "row"), P("seq", "col", "row", None, None)),
        check_vma=False,
    )
```

```python
import jax
import jax.numpy as jnp
from jax import lax
from jax.sharding import PartitionSpec as P

P_SIZE = 64
N = 128


PRECISE = lax.Precision.HIGHEST
EPSILON = 1e-05


def from_behind(value, axis, steps):
    count = lax.axis_size(axis)
    first, last = (max(0, -steps), min(count, count - steps))
    return lax.ppermute(value, axis, [(source, source + steps) for source in range(first, last)])


def local_terms(x_vals, b_proj, c_proj, dt_vals, flag_vals, init_vals, rate_vals):
    rows_here = x_vals.shape[0]
    slot_total = init_vals.shape[0]
    positions = jnp.arange(rows_here, dtype=jnp.int32)
    segment = jnp.cumsum(flag_vals.astype(jnp.int32))
    started = segment[rows_here - 1]
    log_decay = -dt_vals * rate_vals[None, :]
    cumulative = jnp.cumsum(log_decay, axis=0)
    preceding = cumulative - log_decay
    start_at = lax.cummax(jnp.where(flag_vals, positions, 0), axis=0)
    baseline = jnp.where((segment > 0)[:, None], preceding[start_at], 0.0)
    joined = (segment[:, None] == segment[None, :]) & (positions[:, None] >= positions[None, :])
    intersection = jnp.dot(c_proj, b_proj.T, preferred_element_type=jnp.float32)
    cumul_t = cumulative.T
    spread = jnp.where(joined[None], cumul_t[:, :, None] - cumul_t[:, None, :], 0.0)
    mixing = (
        jnp.where(joined[None], jnp.exp(spread), 0.0) * intersection[None] * dt_vals.T[:, None, :]
    )
    internal = jnp.einsum("hij,jhp->ihp", mixing, x_vals.astype(jnp.float32), precision=PRECISE)
    from_slot = jnp.einsum(
        "tn,shpn->tshp", c_proj.astype(jnp.float32), init_vals, precision=PRECISE
    )
    slot_ids = jnp.arange(1, slot_total + 1, dtype=jnp.int32)
    chosen = (segment[:, None] == slot_ids[None, :]).astype(jnp.float32)
    restarted = jnp.einsum("ts,tshp->thp", chosen, from_slot, precision=PRECISE)
    y_part = internal + jnp.exp(cumulative - baseline)[:, :, None] * restarted
    carried = jnp.where((segment == 0)[:, None], jnp.exp(cumulative), 0.0)
    indices = jnp.arange(slot_total + 1, dtype=jnp.int32)
    belongs = segment[:, None] == indices[None, :]
    last_at = jnp.max(jnp.where(belongs, positions[:, None], -1), axis=0)
    first_at = jnp.min(jnp.where(belongs, positions[:, None], rows_here), axis=0)
    cumul_end = jnp.where((last_at >= 0)[:, None], cumulative[jnp.maximum(last_at, 0)], 0.0)
    lag_spread = jnp.where(belongs.T[:, :, None], cumul_end[:, None, :] - cumulative[None], 0.0)
    weights = jnp.where(belongs.T[:, :, None], jnp.exp(lag_spread), 0.0) * dt_vals[None]
    weighted = weights[..., None] * x_vals.astype(jnp.float32)[None]
    gathered = jnp.einsum("sthp,tn->shpn", weighted, b_proj.astype(jnp.float32), precision=PRECISE)
    base_slot = preceding[jnp.minimum(first_at, rows_here - 1)]
    factor = jnp.exp(jnp.where((slot_ids <= started)[:, None], cumul_end[1:] - base_slot[1:], 0.0))
    in_use = slot_ids <= started
    seg_rest = gathered[1:] + jnp.where(
        in_use[:, None, None, None], factor[..., None, None] * init_vals, 0.0
    )
    seg_ends = jnp.concatenate([gathered[:1], seg_rest], axis=0)
    decay_all = jnp.where(started == 0, jnp.exp(cumulative[rows_here - 1]), 0.0)
    state_add = jnp.sum(jnp.where((indices == started)[:, None, None, None], seg_ends, 0.0), axis=0)
    return (y_part, carried, seg_ends, decay_all, state_add, cumul_end[0], started)


def tail_rows(raw, edges, start_last, segment_last, lagged):
    rows_here = raw.shape[0]
    source = jnp.arange(rows_here - lagged, rows_here, dtype=jnp.int32)
    inside = source >= start_last
    row_pick = jnp.clip(lagged - start_last + source, 0, lagged - 1)
    from_edge = edges[jnp.maximum(segment_last - 1, 0), row_pick]
    return jnp.where(inside[:, None], raw[rows_here - lagged :], from_edge)


def convolve(raw, prior, edges, kernel, offset_bias, start_at, segment, positions, lagged):
    rows_here = raw.shape[0]
    slot_total = edges.shape[0]
    extended = jnp.concatenate([prior, raw], axis=0)
    table = edges.reshape(slot_total * lagged, edges.shape[-1])
    total = offset_bias[None].astype(jnp.float32) + kernel[lagged][None].astype(
        jnp.float32
    ) * raw.astype(jnp.float32)
    for offset in range(1, lagged + 1):
        source = positions - offset
        inside = source >= start_at
        row_pick = jnp.clip(lagged - start_at + source, 0, lagged - 1)
        which = jnp.maximum(segment - 1, 0) * lagged + row_pick
        picker = (
            which[:, None] == jnp.arange(slot_total * lagged, dtype=jnp.int32)[None, :]
        ).astype(jnp.bfloat16)
        from_edge = jnp.dot(picker, table, preferred_element_type=jnp.float32)
        earlier = extended[lagged - offset : lagged - offset + rows_here].astype(jnp.float32)
        total = total + kernel[lagged - offset][None].astype(jnp.float32) * jnp.where(
            inside[:, None], earlier, from_edge
        )
    return jax.nn.silu(total).astype(jnp.bfloat16)


def shards(
    hidden,
    w_x,
    w_z,
    w_bc,
    w_dt,
    conv_x_w,
    conv_bc_w,
    conv_x_bias,
    conv_bc_bias,
    dt_bias,
    decay_rate,
    d_skip,
    norm_gain,
    starts,
    init_states,
    conv_x_edges,
    conv_bc_edges,
):
    tokens = lax.all_gather(hidden, "row", axis=0, tiled=True)
    rows_here = tokens.shape[0]
    channels = w_x.shape[2]
    heads_here = w_dt.shape[2]
    lagged = conv_x_w.shape[0] - 1
    x_part, z_part, bc_part, dt_part = [
        jnp.einsum("td,dgc->gtc", tokens, weight, preferred_element_type=jnp.float32)
        for weight in (w_x, w_z, w_bc, w_dt)
    ]
    first = lax.psum_scatter(
        jnp.concatenate([x_part, bc_part, dt_part], axis=2), "col", scatter_dimension=0, tiled=True
    )[0].astype(jnp.bfloat16)
    first, z_part = lax.optimization_barrier((first, z_part))
    z_gate = lax.optimization_barrier(
        lax.psum_scatter(z_part, "col", scatter_dimension=0, tiled=True)[0].astype(jnp.bfloat16)
    )
    x_raw = first[:, :channels]
    bc_raw = first[:, channels : channels + 2 * N]
    dt_raw = first[:, channels + 2 * N :]
    positions = jnp.arange(rows_here, dtype=jnp.int32)
    flag_vals = starts == 1
    segment = jnp.cumsum(starts)
    start_at = lax.cummax(jnp.where(flag_vals, positions, -lagged), axis=0)
    x_edges = conv_x_edges[:, :, 0]
    bc_edges = conv_bc_edges[:, :, 0]
    start_last = start_at[rows_here - 1]
    segment_last = segment[rows_here - 1]
    send_x = tail_rows(x_raw, x_edges, start_last, segment_last, lagged)
    send_bc = tail_rows(bc_raw, bc_edges, start_last, segment_last, lagged)
    prior_x, prior_bc = from_behind((send_x, send_bc), "seq", 1)
    x_conv = convolve(
        x_raw,
        prior_x,
        x_edges,
        conv_x_w[:, 0],
        conv_x_bias[0],
        start_at,
        segment,
        positions,
        lagged,
    )
    bc_conv = convolve(
        bc_raw,
        prior_bc,
        bc_edges,
        conv_bc_w[:, 0],
        conv_bc_bias[0],
        start_at,
        segment,
        positions,
        lagged,
    )
    x_heads = x_conv.reshape(rows_here, heads_here, P_SIZE)
    b_proj = bc_conv[:, :N]
    c_proj = bc_conv[:, N:]
    dt_vals = jax.nn.softplus(dt_raw.astype(jnp.float32) + dt_bias[0][None, :])
    init_vals = init_states[:, 0]
    y_part, carried, seg_ends, decay_all, state_add, end_zero, started = local_terms(
        x_heads, b_proj, c_proj, dt_vals, flag_vals, init_vals, decay_rate[0]
    )

    seq_count = lax.axis_size("seq")
    seq_at = lax.axis_index("seq")
    heads_n, p_n, n_n = state_add.shape
    ones = jnp.ones((heads_n,), jnp.float32)
    zeros_state = jnp.zeros_like(state_add)
    has_start = jnp.where(started > 0, 1.0, 0.0).astype(jnp.float32)

    def pack(decay, state, mark):
        aux = jnp.concatenate(
            [
                jnp.broadcast_to(decay[:, None], (heads_n, n_n // 2)),
                jnp.broadcast_to(mark, (heads_n, n_n - n_n // 2)),
            ],
            axis=1,
        )
        return jnp.concatenate([state, aux[:, None, :]], axis=1)

    def unpack(packed):
        return packed[:, p_n, 0], packed[:, :p_n], packed[0, p_n, n_n - 1]

    fwd_in = (decay_all * ones, state_add)
    fwd_ex = (ones, zeros_state)
    bwd_in = (jnp.exp(end_zero), seg_ends[0], has_start)
    bwd_ex = (ones, zeros_state, jnp.zeros((), jnp.float32))
    shift = 1
    while shift < seq_count:
        last = 2 * shift >= seq_count
        got_f = from_behind(pack(fwd_in[0], fwd_in[1], 0.0), "seq", shift)
        got_b = from_behind(pack(*bwd_in), "seq", -shift)
        early_a, early_b, _ = unpack(got_f)
        late_a, late_b, late_m = unpack(got_b)
        late_ok = seq_at + shift < seq_count
        fwd_ex = (
            fwd_ex[0] * early_a,
            fwd_ex[0][:, None, None] * early_b + fwd_ex[1],
        )

        def near_far(near, far_a, far_b, far_m):
            keep = (near[2] > 0.5) | jnp.logical_not(late_ok)
            return (
                jnp.where(keep, near[0], far_a * near[0]),
                jnp.where(keep, near[1], far_a[:, None, None] * near[1] + far_b),
                jnp.where(keep, near[2], far_m),
            )

        bwd_ex = near_far(bwd_ex, late_a, late_b, late_m)
        if not last:
            fwd_in = (
                fwd_in[0] * early_a,
                fwd_in[0][:, None, None] * early_b + fwd_in[1],
            )
            bwd_in = near_far(bwd_in, late_a, late_b, late_m)
        fwd_in, fwd_ex, bwd_in, bwd_ex = lax.optimization_barrier((fwd_in, fwd_ex, bwd_in, bwd_ex))
        shift *= 2
    state_in = fwd_ex[1]
    carried_in = jnp.einsum("tn,hpn->thp", c_proj.astype(jnp.float32), state_in, precision=PRECISE)
    y_full = (
        y_part
        + carried[:, :, None] * carried_in
        + d_skip[0][None, :, None] * x_heads.astype(jnp.float32)
    )
    tail_state = bwd_ex[0][:, None, None] * state_add + bwd_ex[1]
    slot_ids = jnp.arange(1, init_vals.shape[0] + 1, dtype=jnp.int32)
    finals = jnp.where(
        (slot_ids < started)[:, None, None, None],
        seg_ends[1:],
        jnp.where((slot_ids == started)[:, None, None, None], tail_state[None], 0.0),
    )
    gated = y_full.reshape(rows_here, channels) * jax.nn.silu(z_gate.astype(jnp.float32))
    partial_sq = jnp.sum(gated * gated, axis=-1)
    total_sq = lax.psum(partial_sq, "row")
    mean_sq = total_sq / (channels * lax.axis_size("row"))
    gated_out = (gated * lax.rsqrt(mean_sq + EPSILON)[:, None] * norm_gain[0][None, :]).astype(
        jnp.bfloat16
    )
    return (gated_out.reshape(rows_here, 1, channels), finals[:, None])


def solution(mesh):
    placed = (
        P(("seq", "row"), "col"),
        P("col", None, "row"),
        P("col", None, "row"),
        P("col", None, None),
        P("col", None, "row"),
        P(None, "col", "row"),
        P(None, "col", None),
        P("col", "row"),
        P("col", None),
        P("col", "row"),
        P("col", "row"),
        P("col", "row"),
        P("col", "row"),
        P("seq"),
        P("seq", "col", "row", None, None),
        P("seq", None, "col", "row"),
        P("seq", None, "col", None),
    )
    return jax.shard_map(
        shards,
        mesh=mesh,
        in_specs=placed,
        out_specs=(P("seq", "col", "row"), P("seq", "col", "row", None, None)),
        check_vma=False,
    )
```

```python
import jax
import jax.numpy as jnp
from jax import lax
from jax.sharding import PartitionSpec as P

P_SIZE = 64
N = 128


PRECISE = lax.Precision.HIGHEST
EPSILON = 1e-05


def from_behind(value, axis, steps):
    count = lax.axis_size(axis)
    first, last = (max(0, -steps), min(count, count - steps))
    return lax.ppermute(value, axis, [(source, source + steps) for source in range(first, last)])


def local_terms(x_vals, b_proj, c_proj, dt_vals, flag_vals, init_vals, rate_vals):
    rows_here = x_vals.shape[0]
    slot_total = init_vals.shape[0]
    positions = jnp.arange(rows_here, dtype=jnp.int32)
    segment = jnp.cumsum(flag_vals.astype(jnp.int32))
    started = segment[rows_here - 1]
    log_decay = -dt_vals * rate_vals[None, :]
    cumulative = jnp.cumsum(log_decay, axis=0)
    preceding = cumulative - log_decay
    start_at = lax.cummax(jnp.where(flag_vals, positions, 0), axis=0)
    baseline = jnp.where((segment > 0)[:, None], preceding[start_at], 0.0)
    joined = (segment[:, None] == segment[None, :]) & (positions[:, None] >= positions[None, :])
    intersection = jnp.dot(c_proj, b_proj.T, preferred_element_type=jnp.float32)
    cumul_t = cumulative.T
    spread = jnp.where(joined[None], cumul_t[:, :, None] - cumul_t[:, None, :], 0.0)
    mixing = (
        jnp.where(joined[None], jnp.exp(spread), 0.0) * intersection[None] * dt_vals.T[:, None, :]
    )
    internal = jnp.einsum("hij,jhp->ihp", mixing, x_vals.astype(jnp.float32), precision=PRECISE)
    from_slot = jnp.einsum(
        "tn,shpn->tshp", c_proj.astype(jnp.float32), init_vals, precision=PRECISE
    )
    slot_ids = jnp.arange(1, slot_total + 1, dtype=jnp.int32)
    chosen = (segment[:, None] == slot_ids[None, :]).astype(jnp.float32)
    restarted = jnp.einsum("ts,tshp->thp", chosen, from_slot, precision=PRECISE)
    y_part = internal + jnp.exp(cumulative - baseline)[:, :, None] * restarted
    carried = jnp.where((segment == 0)[:, None], jnp.exp(cumulative), 0.0)
    indices = jnp.arange(slot_total + 1, dtype=jnp.int32)
    belongs = segment[:, None] == indices[None, :]
    last_at = jnp.max(jnp.where(belongs, positions[:, None], -1), axis=0)
    first_at = jnp.min(jnp.where(belongs, positions[:, None], rows_here), axis=0)
    cumul_end = jnp.where((last_at >= 0)[:, None], cumulative[jnp.maximum(last_at, 0)], 0.0)
    lag_spread = jnp.where(belongs.T[:, :, None], cumul_end[:, None, :] - cumulative[None], 0.0)
    weights = jnp.where(belongs.T[:, :, None], jnp.exp(lag_spread), 0.0) * dt_vals[None]
    weighted = weights[..., None] * x_vals.astype(jnp.float32)[None]
    gathered = jnp.einsum("sthp,tn->shpn", weighted, b_proj.astype(jnp.float32), precision=PRECISE)
    base_slot = preceding[jnp.minimum(first_at, rows_here - 1)]
    factor = jnp.exp(jnp.where((slot_ids <= started)[:, None], cumul_end[1:] - base_slot[1:], 0.0))
    in_use = slot_ids <= started
    seg_rest = gathered[1:] + jnp.where(
        in_use[:, None, None, None], factor[..., None, None] * init_vals, 0.0
    )
    seg_ends = jnp.concatenate([gathered[:1], seg_rest], axis=0)
    decay_all = jnp.where(started == 0, jnp.exp(cumulative[rows_here - 1]), 0.0)
    state_add = jnp.sum(jnp.where((indices == started)[:, None, None, None], seg_ends, 0.0), axis=0)
    return (y_part, carried, seg_ends, decay_all, state_add, cumul_end[0], started)


def tail_rows(raw, edges, start_last, segment_last, lagged):
    rows_here = raw.shape[0]
    source = jnp.arange(rows_here - lagged, rows_here, dtype=jnp.int32)
    inside = source >= start_last
    row_pick = jnp.clip(lagged - start_last + source, 0, lagged - 1)
    from_edge = edges[jnp.maximum(segment_last - 1, 0), row_pick]
    return jnp.where(inside[:, None], raw[rows_here - lagged :], from_edge)


def convolve(raw, prior, edges, kernel, offset_bias, start_at, segment, positions, lagged):
    rows_here = raw.shape[0]
    slot_total = edges.shape[0]
    extended = jnp.concatenate([prior, raw], axis=0)
    table = edges.reshape(slot_total * lagged, edges.shape[-1])
    total = offset_bias[None].astype(jnp.float32) + kernel[lagged][None].astype(
        jnp.float32
    ) * raw.astype(jnp.float32)
    for offset in range(1, lagged + 1):
        source = positions - offset
        inside = source >= start_at
        row_pick = jnp.clip(lagged - start_at + source, 0, lagged - 1)
        which = jnp.maximum(segment - 1, 0) * lagged + row_pick
        picker = (
            which[:, None] == jnp.arange(slot_total * lagged, dtype=jnp.int32)[None, :]
        ).astype(jnp.bfloat16)
        from_edge = jnp.dot(picker, table, preferred_element_type=jnp.float32)
        earlier = extended[lagged - offset : lagged - offset + rows_here].astype(jnp.float32)
        total = total + kernel[lagged - offset][None].astype(jnp.float32) * jnp.where(
            inside[:, None], earlier, from_edge
        )
    return jax.nn.silu(total).astype(jnp.bfloat16)


def shards(
    hidden,
    w_x,
    w_z,
    w_bc,
    w_dt,
    conv_x_w,
    conv_bc_w,
    conv_x_bias,
    conv_bc_bias,
    dt_bias,
    decay_rate,
    d_skip,
    norm_gain,
    starts,
    init_states,
    conv_x_edges,
    conv_bc_edges,
):
    other = lax.ppermute(hidden, "row", [(0, 1), (1, 0)])
    row_first = lax.axis_index("row") == 0
    tokens = jnp.concatenate(
        [jnp.where(row_first, hidden, other), jnp.where(row_first, other, hidden)], axis=0
    )
    rows_here = tokens.shape[0]
    channels = w_x.shape[2]
    heads_here = w_dt.shape[2]
    lagged = conv_x_w.shape[0] - 1
    x_part, z_part, bc_part, dt_part = [
        jnp.einsum("td,dgc->gtc", tokens, weight, preferred_element_type=jnp.float32)
        for weight in (w_x, w_z, w_bc, w_dt)
    ]
    first = lax.psum_scatter(
        jnp.concatenate([x_part, bc_part, dt_part], axis=2), "col", scatter_dimension=0, tiled=True
    )[0].astype(jnp.bfloat16)
    first, z_part = lax.optimization_barrier((first, z_part))
    z_gate = lax.optimization_barrier(
        lax.psum_scatter(z_part, "col", scatter_dimension=0, tiled=True)[0].astype(jnp.bfloat16)
    )
    x_raw = first[:, :channels]
    bc_raw = first[:, channels : channels + 2 * N]
    dt_raw = first[:, channels + 2 * N :]
    positions = jnp.arange(rows_here, dtype=jnp.int32)
    flag_vals = starts == 1
    segment = jnp.cumsum(starts)
    start_at = lax.cummax(jnp.where(flag_vals, positions, -lagged), axis=0)
    x_edges = conv_x_edges[:, :, 0]
    bc_edges = conv_bc_edges[:, :, 0]
    start_last = start_at[rows_here - 1]
    segment_last = segment[rows_here - 1]
    send_x = tail_rows(x_raw, x_edges, start_last, segment_last, lagged)
    send_bc = tail_rows(bc_raw, bc_edges, start_last, segment_last, lagged)
    prior_x, prior_bc = from_behind((send_x, send_bc), "seq", 1)
    x_conv = convolve(
        x_raw,
        prior_x,
        x_edges,
        conv_x_w[:, 0],
        conv_x_bias[0],
        start_at,
        segment,
        positions,
        lagged,
    )
    bc_conv = convolve(
        bc_raw,
        prior_bc,
        bc_edges,
        conv_bc_w[:, 0],
        conv_bc_bias[0],
        start_at,
        segment,
        positions,
        lagged,
    )
    x_heads = x_conv.reshape(rows_here, heads_here, P_SIZE)
    b_proj = bc_conv[:, :N]
    c_proj = bc_conv[:, N:]
    dt_vals = jax.nn.softplus(dt_raw.astype(jnp.float32) + dt_bias[0][None, :])
    init_vals = init_states[:, 0]
    y_part, carried, seg_ends, decay_all, state_add, end_zero, started = local_terms(
        x_heads, b_proj, c_proj, dt_vals, flag_vals, init_vals, decay_rate[0]
    )

    seq_count = lax.axis_size("seq")
    seq_at = lax.axis_index("seq")
    heads_n, p_n, n_n = state_add.shape
    ones = jnp.ones((heads_n,), jnp.float32)
    zeros_state = jnp.zeros_like(state_add)
    has_start = jnp.where(started > 0, 1.0, 0.0).astype(jnp.float32)

    def pack(decay, state, mark):
        aux = jnp.concatenate(
            [
                jnp.broadcast_to(decay[:, None], (heads_n, n_n // 2)),
                jnp.broadcast_to(mark, (heads_n, n_n - n_n // 2)),
            ],
            axis=1,
        )
        return jnp.concatenate([state, aux[:, None, :]], axis=1)

    def unpack(packed):
        return packed[:, p_n, 0], packed[:, :p_n], packed[0, p_n, n_n - 1]

    fwd_in = (decay_all * ones, state_add)
    fwd_ex = (ones, zeros_state)
    bwd_in = (jnp.exp(end_zero), seg_ends[0], has_start)
    bwd_ex = (ones, zeros_state, jnp.zeros((), jnp.float32))
    shift = 1
    while shift < seq_count:
        last = 2 * shift >= seq_count
        got_f = from_behind(pack(fwd_in[0], fwd_in[1], 0.0), "seq", shift)
        got_b = from_behind(pack(*bwd_in), "seq", -shift)
        early_a, early_b, _ = unpack(got_f)
        late_a, late_b, late_m = unpack(got_b)
        late_ok = seq_at + shift < seq_count
        fwd_ex = (
            fwd_ex[0] * early_a,
            fwd_ex[0][:, None, None] * early_b + fwd_ex[1],
        )

        def near_far(near, far_a, far_b, far_m):
            keep = (near[2] > 0.5) | jnp.logical_not(late_ok)
            return (
                jnp.where(keep, near[0], far_a * near[0]),
                jnp.where(keep, near[1], far_a[:, None, None] * near[1] + far_b),
                jnp.where(keep, near[2], far_m),
            )

        bwd_ex = near_far(bwd_ex, late_a, late_b, late_m)
        if not last:
            fwd_in = (
                fwd_in[0] * early_a,
                fwd_in[0][:, None, None] * early_b + fwd_in[1],
            )
            bwd_in = near_far(bwd_in, late_a, late_b, late_m)
        fwd_in, fwd_ex, bwd_in, bwd_ex = lax.optimization_barrier((fwd_in, fwd_ex, bwd_in, bwd_ex))
        shift *= 2
    state_in = fwd_ex[1]
    carried_in = jnp.einsum("tn,hpn->thp", c_proj.astype(jnp.float32), state_in, precision=PRECISE)
    y_full = (
        y_part
        + carried[:, :, None] * carried_in
        + d_skip[0][None, :, None] * x_heads.astype(jnp.float32)
    )
    tail_state = bwd_ex[0][:, None, None] * state_add + bwd_ex[1]
    slot_ids = jnp.arange(1, init_vals.shape[0] + 1, dtype=jnp.int32)
    finals = jnp.where(
        (slot_ids < started)[:, None, None, None],
        seg_ends[1:],
        jnp.where((slot_ids == started)[:, None, None, None], tail_state[None], 0.0),
    )
    gated = y_full.reshape(rows_here, channels) * jax.nn.silu(z_gate.astype(jnp.float32))
    partial_sq = jnp.sum(gated * gated, axis=-1)
    total_sq = lax.psum(partial_sq, "row")
    mean_sq = total_sq / (channels * lax.axis_size("row"))
    gated_out = (gated * lax.rsqrt(mean_sq + EPSILON)[:, None] * norm_gain[0][None, :]).astype(
        jnp.bfloat16
    )
    return (gated_out.reshape(rows_here, 1, channels), finals[:, None])


def solution(mesh):
    placed = (
        P(("seq", "row"), "col"),
        P("col", None, "row"),
        P("col", None, "row"),
        P("col", None, None),
        P("col", None, "row"),
        P(None, "col", "row"),
        P(None, "col", None),
        P("col", "row"),
        P("col", None),
        P("col", "row"),
        P("col", "row"),
        P("col", "row"),
        P("col", "row"),
        P("seq"),
        P("seq", "col", "row", None, None),
        P("seq", None, "col", "row"),
        P("seq", None, "col", None),
    )
    return jax.shard_map(
        shards,
        mesh=mesh,
        in_specs=placed,
        out_specs=(P("seq", "col", "row"), P("seq", "col", "row", None, None)),
        check_vma=False,
    )
```

```python
import jax
import jax.numpy as jnp
from jax import lax
from jax.sharding import PartitionSpec as P

P_SIZE = 64
N = 128


PRECISE = lax.Precision.HIGHEST
EPSILON = 1e-05


def from_behind(value, axis, steps):
    count = lax.axis_size(axis)
    first, last = (max(0, -steps), min(count, count - steps))
    return lax.ppermute(value, axis, [(source, source + steps) for source in range(first, last)])


def local_terms(x_vals, b_proj, c_proj, dt_vals, flag_vals, init_vals, rate_vals):
    rows_here = x_vals.shape[0]
    slot_total = init_vals.shape[0]
    positions = jnp.arange(rows_here, dtype=jnp.int32)
    segment = jnp.cumsum(flag_vals.astype(jnp.int32))
    started = segment[rows_here - 1]
    log_decay = -dt_vals * rate_vals[None, :]
    cumulative = jnp.cumsum(log_decay, axis=0)
    preceding = cumulative - log_decay
    start_at = lax.cummax(jnp.where(flag_vals, positions, 0), axis=0)
    baseline = jnp.where((segment > 0)[:, None], preceding[start_at], 0.0)
    joined = (segment[:, None] == segment[None, :]) & (positions[:, None] >= positions[None, :])
    intersection = jnp.dot(c_proj, b_proj.T, preferred_element_type=jnp.float32)
    cumul_t = cumulative.T
    spread = jnp.where(joined[None], cumul_t[:, :, None] - cumul_t[:, None, :], 0.0)
    mixing = (
        jnp.where(joined[None], jnp.exp(spread), 0.0) * intersection[None] * dt_vals.T[:, None, :]
    )
    internal = jnp.einsum("hij,jhp->ihp", mixing, x_vals.astype(jnp.float32), precision=PRECISE)
    from_slot = jnp.einsum(
        "tn,shpn->tshp", c_proj.astype(jnp.float32), init_vals, precision=PRECISE
    )
    slot_ids = jnp.arange(1, slot_total + 1, dtype=jnp.int32)
    chosen = (segment[:, None] == slot_ids[None, :]).astype(jnp.float32)
    restarted = jnp.einsum("ts,tshp->thp", chosen, from_slot, precision=PRECISE)
    y_part = internal + jnp.exp(cumulative - baseline)[:, :, None] * restarted
    carried = jnp.where((segment == 0)[:, None], jnp.exp(cumulative), 0.0)
    indices = jnp.arange(slot_total + 1, dtype=jnp.int32)
    belongs = segment[:, None] == indices[None, :]
    last_at = jnp.max(jnp.where(belongs, positions[:, None], -1), axis=0)
    first_at = jnp.min(jnp.where(belongs, positions[:, None], rows_here), axis=0)
    cumul_end = jnp.where((last_at >= 0)[:, None], cumulative[jnp.maximum(last_at, 0)], 0.0)
    lag_spread = jnp.where(belongs.T[:, :, None], cumul_end[:, None, :] - cumulative[None], 0.0)
    weights = jnp.where(belongs.T[:, :, None], jnp.exp(lag_spread), 0.0) * dt_vals[None]
    weighted = weights[..., None] * x_vals.astype(jnp.float32)[None]
    gathered = jnp.einsum("sthp,tn->shpn", weighted, b_proj.astype(jnp.float32), precision=PRECISE)
    base_slot = preceding[jnp.minimum(first_at, rows_here - 1)]
    factor = jnp.exp(jnp.where((slot_ids <= started)[:, None], cumul_end[1:] - base_slot[1:], 0.0))
    in_use = slot_ids <= started
    seg_rest = gathered[1:] + jnp.where(
        in_use[:, None, None, None], factor[..., None, None] * init_vals, 0.0
    )
    seg_ends = jnp.concatenate([gathered[:1], seg_rest], axis=0)
    decay_all = jnp.where(started == 0, jnp.exp(cumulative[rows_here - 1]), 0.0)
    state_add = jnp.sum(jnp.where((indices == started)[:, None, None, None], seg_ends, 0.0), axis=0)
    return (y_part, carried, seg_ends, decay_all, state_add, cumul_end[0], started)


def tail_rows(raw, edges, start_last, segment_last, lagged):
    rows_here = raw.shape[0]
    source = jnp.arange(rows_here - lagged, rows_here, dtype=jnp.int32)
    inside = source >= start_last
    row_pick = jnp.clip(lagged - start_last + source, 0, lagged - 1)
    from_edge = edges[jnp.maximum(segment_last - 1, 0), row_pick]
    return jnp.where(inside[:, None], raw[rows_here - lagged :], from_edge)


def convolve(raw, prior, edges, kernel, offset_bias, start_at, segment, positions, lagged):
    rows_here = raw.shape[0]
    slot_total = edges.shape[0]
    extended = jnp.concatenate([prior, raw], axis=0)
    table = edges.reshape(slot_total * lagged, edges.shape[-1])
    total = offset_bias[None].astype(jnp.float32) + kernel[lagged][None].astype(
        jnp.float32
    ) * raw.astype(jnp.float32)
    for offset in range(1, lagged + 1):
        source = positions - offset
        inside = source >= start_at
        row_pick = jnp.clip(lagged - start_at + source, 0, lagged - 1)
        which = jnp.maximum(segment - 1, 0) * lagged + row_pick
        picker = (
            which[:, None] == jnp.arange(slot_total * lagged, dtype=jnp.int32)[None, :]
        ).astype(jnp.bfloat16)
        from_edge = jnp.dot(picker, table, preferred_element_type=jnp.float32)
        earlier = extended[lagged - offset : lagged - offset + rows_here].astype(jnp.float32)
        total = total + kernel[lagged - offset][None].astype(jnp.float32) * jnp.where(
            inside[:, None], earlier, from_edge
        )
    return jax.nn.silu(total).astype(jnp.bfloat16)


def shards(
    hidden,
    w_x,
    w_z,
    w_bc,
    w_dt,
    conv_x_w,
    conv_bc_w,
    conv_x_bias,
    conv_bc_bias,
    dt_bias,
    decay_rate,
    d_skip,
    norm_gain,
    starts,
    init_states,
    conv_x_edges,
    conv_bc_edges,
):
    other = lax.ppermute(hidden, "row", [(0, 1), (1, 0)])
    row_first = lax.axis_index("row") == 0
    tokens = jnp.concatenate(
        [jnp.where(row_first, hidden, other), jnp.where(row_first, other, hidden)], axis=0
    )
    rows_here = tokens.shape[0]
    channels = w_x.shape[2]
    heads_here = w_dt.shape[2]
    lagged = conv_x_w.shape[0] - 1
    row_at = lax.axis_index("row")
    bc_cols = w_bc.shape[2] // lax.axis_size("row")
    w_bc_mine = lax.dynamic_slice_in_dim(w_bc, row_at * bc_cols, bc_cols, axis=2)
    x_part, z_part, bc_part, dt_part = [
        jnp.einsum("td,dgc->gtc", tokens, weight, preferred_element_type=jnp.float32)
        for weight in (w_x, w_z, w_bc_mine, w_dt)
    ]
    first = lax.psum_scatter(
        jnp.concatenate([x_part, bc_part, dt_part], axis=2), "col", scatter_dimension=0, tiled=True
    )[0].astype(jnp.bfloat16)
    first, z_part = lax.optimization_barrier((first, z_part))
    z_gate = lax.optimization_barrier(
        lax.psum_scatter(z_part, "col", scatter_dimension=0, tiled=True)[0].astype(jnp.bfloat16)
    )
    x_raw = first[:, :channels]
    bc_mine = first[:, channels : channels + bc_cols]
    bc_other = lax.ppermute(bc_mine, "row", [(0, 1), (1, 0)])
    bc_raw = jnp.concatenate(
        [jnp.where(row_first, bc_mine, bc_other), jnp.where(row_first, bc_other, bc_mine)], axis=1
    )
    dt_raw = first[:, channels + bc_cols :]
    positions = jnp.arange(rows_here, dtype=jnp.int32)
    flag_vals = starts == 1
    segment = jnp.cumsum(starts)
    start_at = lax.cummax(jnp.where(flag_vals, positions, -lagged), axis=0)
    x_edges = conv_x_edges[:, :, 0]
    bc_edges = conv_bc_edges[:, :, 0]
    start_last = start_at[rows_here - 1]
    segment_last = segment[rows_here - 1]
    send_x = tail_rows(x_raw, x_edges, start_last, segment_last, lagged)
    send_bc = tail_rows(bc_raw, bc_edges, start_last, segment_last, lagged)
    prior_x, prior_bc = from_behind((send_x, send_bc), "seq", 1)
    x_conv = convolve(
        x_raw,
        prior_x,
        x_edges,
        conv_x_w[:, 0],
        conv_x_bias[0],
        start_at,
        segment,
        positions,
        lagged,
    )
    bc_conv = convolve(
        bc_raw,
        prior_bc,
        bc_edges,
        conv_bc_w[:, 0],
        conv_bc_bias[0],
        start_at,
        segment,
        positions,
        lagged,
    )
    x_heads = x_conv.reshape(rows_here, heads_here, P_SIZE)
    b_proj = bc_conv[:, :N]
    c_proj = bc_conv[:, N:]
    dt_vals = jax.nn.softplus(dt_raw.astype(jnp.float32) + dt_bias[0][None, :])
    init_vals = init_states[:, 0]
    y_part, carried, seg_ends, decay_all, state_add, end_zero, started = local_terms(
        x_heads, b_proj, c_proj, dt_vals, flag_vals, init_vals, decay_rate[0]
    )

    seq_count = lax.axis_size("seq")
    seq_at = lax.axis_index("seq")
    heads_n, p_n, n_n = state_add.shape
    ones = jnp.ones((heads_n,), jnp.float32)
    zeros_state = jnp.zeros_like(state_add)
    has_start = jnp.where(started > 0, 1.0, 0.0).astype(jnp.float32)

    def pack(decay, state, mark):
        aux = jnp.concatenate(
            [
                jnp.broadcast_to(decay[:, None], (heads_n, n_n // 2)),
                jnp.broadcast_to(mark, (heads_n, n_n - n_n // 2)),
            ],
            axis=1,
        )
        return jnp.concatenate([state, aux[:, None, :]], axis=1)

    def unpack(packed):
        return packed[:, p_n, 0], packed[:, :p_n], packed[0, p_n, n_n - 1]

    fwd_in = (decay_all * ones, state_add)
    fwd_ex = (ones, zeros_state)
    bwd_in = (jnp.exp(end_zero), seg_ends[0], has_start)
    bwd_ex = (ones, zeros_state, jnp.zeros((), jnp.float32))
    shift = 1
    while shift < seq_count:
        last = 2 * shift >= seq_count
        got_f = from_behind(pack(fwd_in[0], fwd_in[1], 0.0), "seq", shift)
        got_b = from_behind(pack(*bwd_in), "seq", -shift)
        early_a, early_b, _ = unpack(got_f)
        late_a, late_b, late_m = unpack(got_b)
        late_ok = seq_at + shift < seq_count
        fwd_ex = (
            fwd_ex[0] * early_a,
            fwd_ex[0][:, None, None] * early_b + fwd_ex[1],
        )

        def near_far(near, far_a, far_b, far_m):
            keep = (near[2] > 0.5) | jnp.logical_not(late_ok)
            return (
                jnp.where(keep, near[0], far_a * near[0]),
                jnp.where(keep, near[1], far_a[:, None, None] * near[1] + far_b),
                jnp.where(keep, near[2], far_m),
            )

        bwd_ex = near_far(bwd_ex, late_a, late_b, late_m)
        if not last:
            fwd_in = (
                fwd_in[0] * early_a,
                fwd_in[0][:, None, None] * early_b + fwd_in[1],
            )
            bwd_in = near_far(bwd_in, late_a, late_b, late_m)
        fwd_in, fwd_ex, bwd_in, bwd_ex = lax.optimization_barrier((fwd_in, fwd_ex, bwd_in, bwd_ex))
        shift *= 2
    state_in = fwd_ex[1]
    carried_in = jnp.einsum("tn,hpn->thp", c_proj.astype(jnp.float32), state_in, precision=PRECISE)
    y_full = (
        y_part
        + carried[:, :, None] * carried_in
        + d_skip[0][None, :, None] * x_heads.astype(jnp.float32)
    )
    tail_state = bwd_ex[0][:, None, None] * state_add + bwd_ex[1]
    slot_ids = jnp.arange(1, init_vals.shape[0] + 1, dtype=jnp.int32)
    finals = jnp.where(
        (slot_ids < started)[:, None, None, None],
        seg_ends[1:],
        jnp.where((slot_ids == started)[:, None, None, None], tail_state[None], 0.0),
    )
    gated = y_full.reshape(rows_here, channels) * jax.nn.silu(z_gate.astype(jnp.float32))
    partial_sq = jnp.sum(gated * gated, axis=-1)
    total_sq = lax.psum(partial_sq, "row")
    mean_sq = total_sq / (channels * lax.axis_size("row"))
    gated_out = (gated * lax.rsqrt(mean_sq + EPSILON)[:, None] * norm_gain[0][None, :]).astype(
        jnp.bfloat16
    )
    return (gated_out.reshape(rows_here, 1, channels), finals[:, None])


def solution(mesh):
    placed = (
        P(("seq", "row"), "col"),
        P("col", None, "row"),
        P("col", None, "row"),
        P("col", None, None),
        P("col", None, "row"),
        P(None, "col", "row"),
        P(None, "col", None),
        P("col", "row"),
        P("col", None),
        P("col", "row"),
        P("col", "row"),
        P("col", "row"),
        P("col", "row"),
        P("seq"),
        P("seq", "col", "row", None, None),
        P("seq", None, "col", "row"),
        P("seq", None, "col", None),
    )
    return jax.shard_map(
        shards,
        mesh=mesh,
        in_specs=placed,
        out_specs=(P("seq", "col", "row"), P("seq", "col", "row", None, None)),
        check_vma=False,
    )
```

```python
import jax
import jax.numpy as jnp
from jax import lax
from jax.sharding import PartitionSpec as P

P_SIZE = 64
N = 128


PRECISE = lax.Precision.HIGHEST
EPSILON = 1e-05


def from_behind(value, axis, steps):
    count = lax.axis_size(axis)
    first, last = (max(0, -steps), min(count, count - steps))
    return lax.ppermute(value, axis, [(source, source + steps) for source in range(first, last)])


def local_terms(x_vals, b_proj, c_proj, dt_vals, flag_vals, init_vals, rate_vals):
    rows_here = x_vals.shape[0]
    slot_total = init_vals.shape[0]
    positions = jnp.arange(rows_here, dtype=jnp.int32)
    segment = jnp.cumsum(flag_vals.astype(jnp.int32))
    started = segment[rows_here - 1]
    log_decay = -dt_vals * rate_vals[None, :]
    cumulative = jnp.cumsum(log_decay, axis=0)
    preceding = cumulative - log_decay
    start_at = lax.cummax(jnp.where(flag_vals, positions, 0), axis=0)
    baseline = jnp.where((segment > 0)[:, None], preceding[start_at], 0.0)
    joined = (segment[:, None] == segment[None, :]) & (positions[:, None] >= positions[None, :])
    intersection = jnp.dot(c_proj, b_proj.T, preferred_element_type=jnp.float32)
    cumul_t = cumulative.T
    spread = jnp.where(joined[None], cumul_t[:, :, None] - cumul_t[:, None, :], 0.0)
    mixing = (
        jnp.where(joined[None], jnp.exp(spread), 0.0) * intersection[None] * dt_vals.T[:, None, :]
    )
    internal = jnp.einsum("hij,jhp->ihp", mixing, x_vals.astype(jnp.float32), precision=PRECISE)
    from_slot = jnp.einsum(
        "tn,shpn->tshp", c_proj.astype(jnp.float32), init_vals, precision=PRECISE
    )
    slot_ids = jnp.arange(1, slot_total + 1, dtype=jnp.int32)
    chosen = (segment[:, None] == slot_ids[None, :]).astype(jnp.float32)
    restarted = jnp.einsum("ts,tshp->thp", chosen, from_slot, precision=PRECISE)
    y_part = internal + jnp.exp(cumulative - baseline)[:, :, None] * restarted
    carried = jnp.where((segment == 0)[:, None], jnp.exp(cumulative), 0.0)
    indices = jnp.arange(slot_total + 1, dtype=jnp.int32)
    belongs = segment[:, None] == indices[None, :]
    last_at = jnp.max(jnp.where(belongs, positions[:, None], -1), axis=0)
    first_at = jnp.min(jnp.where(belongs, positions[:, None], rows_here), axis=0)
    cumul_end = jnp.where((last_at >= 0)[:, None], cumulative[jnp.maximum(last_at, 0)], 0.0)
    lag_spread = jnp.where(belongs.T[:, :, None], cumul_end[:, None, :] - cumulative[None], 0.0)
    weights = jnp.where(belongs.T[:, :, None], jnp.exp(lag_spread), 0.0) * dt_vals[None]
    weighted = weights[..., None] * x_vals.astype(jnp.float32)[None]
    gathered = jnp.einsum("sthp,tn->shpn", weighted, b_proj.astype(jnp.float32), precision=PRECISE)
    base_slot = preceding[jnp.minimum(first_at, rows_here - 1)]
    factor = jnp.exp(jnp.where((slot_ids <= started)[:, None], cumul_end[1:] - base_slot[1:], 0.0))
    in_use = slot_ids <= started
    seg_rest = gathered[1:] + jnp.where(
        in_use[:, None, None, None], factor[..., None, None] * init_vals, 0.0
    )
    seg_ends = jnp.concatenate([gathered[:1], seg_rest], axis=0)
    decay_all = jnp.where(started == 0, jnp.exp(cumulative[rows_here - 1]), 0.0)
    state_add = jnp.sum(jnp.where((indices == started)[:, None, None, None], seg_ends, 0.0), axis=0)
    return (y_part, carried, seg_ends, decay_all, state_add, cumul_end[0], started)


def tail_rows(raw, edges, start_last, segment_last, lagged):
    rows_here = raw.shape[0]
    source = jnp.arange(rows_here - lagged, rows_here, dtype=jnp.int32)
    inside = source >= start_last
    row_pick = jnp.clip(lagged - start_last + source, 0, lagged - 1)
    from_edge = edges[jnp.maximum(segment_last - 1, 0), row_pick]
    return jnp.where(inside[:, None], raw[rows_here - lagged :], from_edge)


def convolve(raw, prior, edges, kernel, offset_bias, start_at, segment, positions, lagged):
    rows_here = raw.shape[0]
    slot_total = edges.shape[0]
    extended = jnp.concatenate([prior, raw], axis=0)
    table = edges.reshape(slot_total * lagged, edges.shape[-1])
    total = offset_bias[None].astype(jnp.float32) + kernel[lagged][None].astype(
        jnp.float32
    ) * raw.astype(jnp.float32)
    for offset in range(1, lagged + 1):
        source = positions - offset
        inside = source >= start_at
        row_pick = jnp.clip(lagged - start_at + source, 0, lagged - 1)
        which = jnp.maximum(segment - 1, 0) * lagged + row_pick
        picker = (
            which[:, None] == jnp.arange(slot_total * lagged, dtype=jnp.int32)[None, :]
        ).astype(jnp.bfloat16)
        from_edge = jnp.dot(picker, table, preferred_element_type=jnp.float32)
        earlier = extended[lagged - offset : lagged - offset + rows_here].astype(jnp.float32)
        total = total + kernel[lagged - offset][None].astype(jnp.float32) * jnp.where(
            inside[:, None], earlier, from_edge
        )
    return jax.nn.silu(total).astype(jnp.bfloat16)


def shards(
    hidden,
    w_x,
    w_z,
    w_bc,
    w_dt,
    conv_x_w,
    conv_bc_w,
    conv_x_bias,
    conv_bc_bias,
    dt_bias,
    decay_rate,
    d_skip,
    norm_gain,
    starts,
    init_states,
    conv_x_edges,
    conv_bc_edges,
):
    other = lax.ppermute(hidden, "row", [(0, 1), (1, 0)])
    row_first = lax.axis_index("row") == 0
    tokens = jnp.concatenate(
        [jnp.where(row_first, hidden, other), jnp.where(row_first, other, hidden)], axis=0
    )
    rows_here = tokens.shape[0]
    channels = w_x.shape[2]
    heads_here = w_dt.shape[2]
    lagged = conv_x_w.shape[0] - 1
    row_at = lax.axis_index("row")
    bc_cols = w_bc.shape[2] // lax.axis_size("row")
    w_bc_mine = lax.dynamic_slice_in_dim(w_bc, row_at * bc_cols, bc_cols, axis=2)
    x_part, z_part, bc_part, dt_part = [
        jnp.einsum("td,dgc->gtc", tokens, weight, preferred_element_type=jnp.float32)
        for weight in (w_x, w_z, w_bc_mine, w_dt)
    ]
    first = lax.psum_scatter(
        jnp.concatenate([x_part, bc_part, dt_part], axis=2), "col", scatter_dimension=0, tiled=True
    )[0].astype(jnp.bfloat16)
    first, z_part = lax.optimization_barrier((first, z_part))
    z_gate = lax.optimization_barrier(
        lax.psum_scatter(z_part, "col", scatter_dimension=0, tiled=True)[0].astype(jnp.bfloat16)
    )
    x_raw = first[:, :channels]
    bc_mine = first[:, channels : channels + bc_cols]
    bc_other = lax.ppermute(bc_mine, "row", [(0, 1), (1, 0)])
    bc_raw = jnp.concatenate(
        [jnp.where(row_first, bc_mine, bc_other), jnp.where(row_first, bc_other, bc_mine)], axis=1
    )
    dt_raw = first[:, channels + bc_cols :]
    positions = jnp.arange(rows_here, dtype=jnp.int32)
    flag_vals = starts == 1
    segment = jnp.cumsum(starts)
    start_at = lax.cummax(jnp.where(flag_vals, positions, -lagged), axis=0)
    x_edges = conv_x_edges[:, :, 0]
    bc_edges = conv_bc_edges[:, :, 0]
    start_last = start_at[rows_here - 1]
    segment_last = segment[rows_here - 1]
    send_x = tail_rows(x_raw, x_edges, start_last, segment_last, lagged)
    send_bc = tail_rows(bc_raw, bc_edges, start_last, segment_last, lagged)
    prior_both = from_behind(jnp.concatenate([send_x, send_bc], axis=1), "seq", 1)
    prior_x = prior_both[:, :channels]
    prior_bc = prior_both[:, channels:]
    x_conv = convolve(
        x_raw,
        prior_x,
        x_edges,
        conv_x_w[:, 0],
        conv_x_bias[0],
        start_at,
        segment,
        positions,
        lagged,
    )
    bc_conv = convolve(
        bc_raw,
        prior_bc,
        bc_edges,
        conv_bc_w[:, 0],
        conv_bc_bias[0],
        start_at,
        segment,
        positions,
        lagged,
    )
    x_heads = x_conv.reshape(rows_here, heads_here, P_SIZE)
    b_proj = bc_conv[:, :N]
    c_proj = bc_conv[:, N:]
    dt_vals = jax.nn.softplus(dt_raw.astype(jnp.float32) + dt_bias[0][None, :])
    init_vals = init_states[:, 0]
    y_part, carried, seg_ends, decay_all, state_add, end_zero, started = local_terms(
        x_heads, b_proj, c_proj, dt_vals, flag_vals, init_vals, decay_rate[0]
    )

    seq_count = lax.axis_size("seq")
    seq_at = lax.axis_index("seq")
    heads_n, p_n, n_n = state_add.shape
    ones = jnp.ones((heads_n,), jnp.float32)
    zeros_state = jnp.zeros_like(state_add)
    has_start = jnp.where(started > 0, 1.0, 0.0).astype(jnp.float32)

    def pack(decay, state, mark):
        aux = jnp.concatenate(
            [
                jnp.broadcast_to(decay[:, None], (heads_n, n_n // 2)),
                jnp.broadcast_to(mark, (heads_n, n_n - n_n // 2)),
            ],
            axis=1,
        )
        return jnp.concatenate([state, aux[:, None, :]], axis=1)

    def unpack(packed):
        return packed[:, p_n, 0], packed[:, :p_n], packed[0, p_n, n_n - 1]

    fwd_in = (decay_all * ones, state_add)
    fwd_ex = (ones, zeros_state)
    bwd_in = (jnp.exp(end_zero), seg_ends[0], has_start)
    bwd_ex = (ones, zeros_state, jnp.zeros((), jnp.float32))
    shift = 1
    while shift < seq_count:
        last = 2 * shift >= seq_count
        got_f = from_behind(pack(fwd_in[0], fwd_in[1], 0.0), "seq", shift)
        got_b = from_behind(pack(*bwd_in), "seq", -shift)
        early_a, early_b, _ = unpack(got_f)
        late_a, late_b, late_m = unpack(got_b)
        late_ok = seq_at + shift < seq_count
        fwd_ex = (
            fwd_ex[0] * early_a,
            fwd_ex[0][:, None, None] * early_b + fwd_ex[1],
        )

        def near_far(near, far_a, far_b, far_m):
            keep = (near[2] > 0.5) | jnp.logical_not(late_ok)
            return (
                jnp.where(keep, near[0], far_a * near[0]),
                jnp.where(keep, near[1], far_a[:, None, None] * near[1] + far_b),
                jnp.where(keep, near[2], far_m),
            )

        bwd_ex = near_far(bwd_ex, late_a, late_b, late_m)
        if not last:
            fwd_in = (
                fwd_in[0] * early_a,
                fwd_in[0][:, None, None] * early_b + fwd_in[1],
            )
            bwd_in = near_far(bwd_in, late_a, late_b, late_m)
        fwd_in, fwd_ex, bwd_in, bwd_ex = lax.optimization_barrier((fwd_in, fwd_ex, bwd_in, bwd_ex))
        shift *= 2
    state_in = fwd_ex[1]
    carried_in = jnp.einsum("tn,hpn->thp", c_proj.astype(jnp.float32), state_in, precision=PRECISE)
    y_full = (
        y_part
        + carried[:, :, None] * carried_in
        + d_skip[0][None, :, None] * x_heads.astype(jnp.float32)
    )
    tail_state = bwd_ex[0][:, None, None] * state_add + bwd_ex[1]
    slot_ids = jnp.arange(1, init_vals.shape[0] + 1, dtype=jnp.int32)
    finals = jnp.where(
        (slot_ids < started)[:, None, None, None],
        seg_ends[1:],
        jnp.where((slot_ids == started)[:, None, None, None], tail_state[None], 0.0),
    )
    gated = y_full.reshape(rows_here, channels) * jax.nn.silu(z_gate.astype(jnp.float32))
    partial_sq = jnp.sum(gated * gated, axis=-1)
    total_sq = lax.psum(partial_sq, "row")
    mean_sq = total_sq / (channels * lax.axis_size("row"))
    gated_out = (gated * lax.rsqrt(mean_sq + EPSILON)[:, None] * norm_gain[0][None, :]).astype(
        jnp.bfloat16
    )
    return (gated_out.reshape(rows_here, 1, channels), finals[:, None])


def solution(mesh):
    placed = (
        P(("seq", "row"), "col"),
        P("col", None, "row"),
        P("col", None, "row"),
        P("col", None, None),
        P("col", None, "row"),
        P(None, "col", "row"),
        P(None, "col", None),
        P("col", "row"),
        P("col", None),
        P("col", "row"),
        P("col", "row"),
        P("col", "row"),
        P("col", "row"),
        P("seq"),
        P("seq", "col", "row", None, None),
        P("seq", None, "col", "row"),
        P("seq", None, "col", None),
    )
    return jax.shard_map(
        shards,
        mesh=mesh,
        in_specs=placed,
        out_specs=(P("seq", "col", "row"), P("seq", "col", "row", None, None)),
        check_vma=False,
    )
```

```python
import jax
import jax.numpy as jnp
from jax import lax
from jax.sharding import PartitionSpec as P

P_SIZE = 64
N = 128


PRECISE = lax.Precision.HIGHEST
EPSILON = 1e-05


def from_behind(value, axis, steps):
    count = lax.axis_size(axis)
    first, last = (max(0, -steps), min(count, count - steps))
    return lax.ppermute(value, axis, [(source, source + steps) for source in range(first, last)])


def local_terms(x_vals, b_proj, c_proj, dt_vals, flag_vals, init_vals, rate_vals):
    rows_here = x_vals.shape[0]
    slot_total = init_vals.shape[0]
    positions = jnp.arange(rows_here, dtype=jnp.int32)
    segment = jnp.cumsum(flag_vals.astype(jnp.int32))
    started = segment[rows_here - 1]
    log_decay = -dt_vals * rate_vals[None, :]
    cumulative = jnp.cumsum(log_decay, axis=0)
    preceding = cumulative - log_decay
    start_at = lax.cummax(jnp.where(flag_vals, positions, 0), axis=0)
    baseline = jnp.where((segment > 0)[:, None], preceding[start_at], 0.0)
    joined = (segment[:, None] == segment[None, :]) & (positions[:, None] >= positions[None, :])
    intersection = jnp.dot(c_proj, b_proj.T, preferred_element_type=jnp.float32)
    cumul_t = cumulative.T
    spread = jnp.where(joined[None], cumul_t[:, :, None] - cumul_t[:, None, :], 0.0)
    mixing = (
        jnp.where(joined[None], jnp.exp(spread), 0.0) * intersection[None] * dt_vals.T[:, None, :]
    )
    internal = jnp.einsum("hij,jhp->ihp", mixing, x_vals.astype(jnp.float32), precision=PRECISE)
    from_slot = jnp.einsum(
        "tn,shpn->tshp", c_proj.astype(jnp.float32), init_vals, precision=PRECISE
    )
    slot_ids = jnp.arange(1, slot_total + 1, dtype=jnp.int32)
    chosen = (segment[:, None] == slot_ids[None, :]).astype(jnp.float32)
    restarted = jnp.einsum("ts,tshp->thp", chosen, from_slot, precision=PRECISE)
    y_part = internal + jnp.exp(cumulative - baseline)[:, :, None] * restarted
    carried = jnp.where((segment == 0)[:, None], jnp.exp(cumulative), 0.0)
    indices = jnp.arange(slot_total + 1, dtype=jnp.int32)
    belongs = segment[:, None] == indices[None, :]
    last_at = jnp.max(jnp.where(belongs, positions[:, None], -1), axis=0)
    first_at = jnp.min(jnp.where(belongs, positions[:, None], rows_here), axis=0)
    cumul_end = jnp.where((last_at >= 0)[:, None], cumulative[jnp.maximum(last_at, 0)], 0.0)
    lag_spread = jnp.where(belongs.T[:, :, None], cumul_end[:, None, :] - cumulative[None], 0.0)
    weights = jnp.where(belongs.T[:, :, None], jnp.exp(lag_spread), 0.0) * dt_vals[None]
    weighted = weights[..., None] * x_vals.astype(jnp.float32)[None]
    gathered = jnp.einsum("sthp,tn->shpn", weighted, b_proj.astype(jnp.float32), precision=PRECISE)
    base_slot = preceding[jnp.minimum(first_at, rows_here - 1)]
    factor = jnp.exp(jnp.where((slot_ids <= started)[:, None], cumul_end[1:] - base_slot[1:], 0.0))
    in_use = slot_ids <= started
    seg_rest = gathered[1:] + jnp.where(
        in_use[:, None, None, None], factor[..., None, None] * init_vals, 0.0
    )
    seg_ends = jnp.concatenate([gathered[:1], seg_rest], axis=0)
    decay_all = jnp.where(started == 0, jnp.exp(cumulative[rows_here - 1]), 0.0)
    state_add = jnp.sum(jnp.where((indices == started)[:, None, None, None], seg_ends, 0.0), axis=0)
    return (y_part, carried, seg_ends, decay_all, state_add, cumul_end[0], started)


def tail_rows(raw, edges, start_last, segment_last, lagged):
    rows_here = raw.shape[0]
    source = jnp.arange(rows_here - lagged, rows_here, dtype=jnp.int32)
    inside = source >= start_last
    row_pick = jnp.clip(lagged - start_last + source, 0, lagged - 1)
    from_edge = edges[jnp.maximum(segment_last - 1, 0), row_pick]
    return jnp.where(inside[:, None], raw[rows_here - lagged :], from_edge)


def convolve(raw, prior, edges, kernel, offset_bias, start_at, segment, positions, lagged):
    rows_here = raw.shape[0]
    slot_total = edges.shape[0]
    extended = jnp.concatenate([prior, raw], axis=0)
    table = edges.reshape(slot_total * lagged, edges.shape[-1])
    total = offset_bias[None].astype(jnp.float32) + kernel[lagged][None].astype(
        jnp.float32
    ) * raw.astype(jnp.float32)
    for offset in range(1, lagged + 1):
        source = positions - offset
        inside = source >= start_at
        row_pick = jnp.clip(lagged - start_at + source, 0, lagged - 1)
        which = jnp.maximum(segment - 1, 0) * lagged + row_pick
        picker = (
            which[:, None] == jnp.arange(slot_total * lagged, dtype=jnp.int32)[None, :]
        ).astype(jnp.bfloat16)
        from_edge = jnp.dot(picker, table, preferred_element_type=jnp.float32)
        earlier = extended[lagged - offset : lagged - offset + rows_here].astype(jnp.float32)
        total = total + kernel[lagged - offset][None].astype(jnp.float32) * jnp.where(
            inside[:, None], earlier, from_edge
        )
    return jax.nn.silu(total).astype(jnp.bfloat16)


def shards(
    hidden,
    w_x,
    w_z,
    w_bc,
    w_dt,
    conv_x_w,
    conv_bc_w,
    conv_x_bias,
    conv_bc_bias,
    dt_bias,
    decay_rate,
    d_skip,
    norm_gain,
    starts,
    init_states,
    conv_x_edges,
    conv_bc_edges,
):
    other = lax.ppermute(hidden, "row", [(0, 1), (1, 0)])
    row_first = lax.axis_index("row") == 0
    tokens = jnp.concatenate(
        [jnp.where(row_first, hidden, other), jnp.where(row_first, other, hidden)], axis=0
    )
    rows_here = tokens.shape[0]
    channels = w_x.shape[2]
    heads_here = w_dt.shape[2]
    lagged = conv_x_w.shape[0] - 1
    row_at = lax.axis_index("row")
    bc_cols = w_bc.shape[2] // lax.axis_size("row")
    w_bc_mine = lax.dynamic_slice_in_dim(w_bc, row_at * bc_cols, bc_cols, axis=2)
    x_part, z_part, bc_part, dt_part = [
        jnp.einsum("td,dgc->gtc", tokens, weight, preferred_element_type=jnp.float32)
        for weight in (w_x, w_z, w_bc_mine, w_dt)
    ]
    first = lax.psum_scatter(
        jnp.concatenate([x_part, bc_part, dt_part], axis=2), "col", scatter_dimension=0, tiled=True
    )[0].astype(jnp.bfloat16)
    first, z_part = lax.optimization_barrier((first, z_part))
    z_gate = lax.optimization_barrier(
        lax.psum_scatter(z_part, "col", scatter_dimension=0, tiled=True)[0].astype(jnp.bfloat16)
    )
    x_raw = first[:, :channels]
    bc_raw = first[:, channels : channels + bc_cols]
    dt_raw = first[:, channels + bc_cols :]
    positions = jnp.arange(rows_here, dtype=jnp.int32)
    flag_vals = starts == 1
    segment = jnp.cumsum(starts)
    start_at = lax.cummax(jnp.where(flag_vals, positions, -lagged), axis=0)
    x_edges = conv_x_edges[:, :, 0]
    bc_edges = lax.dynamic_slice_in_dim(conv_bc_edges[:, :, 0], row_at * bc_cols, bc_cols, axis=2)
    start_last = start_at[rows_here - 1]
    segment_last = segment[rows_here - 1]
    send_x = tail_rows(x_raw, x_edges, start_last, segment_last, lagged)
    send_bc = tail_rows(bc_raw, bc_edges, start_last, segment_last, lagged)
    prior_both = from_behind(jnp.concatenate([send_x, send_bc], axis=1), "seq", 1)
    prior_x = prior_both[:, :channels]
    prior_bc = prior_both[:, channels:]
    x_conv = convolve(
        x_raw,
        prior_x,
        x_edges,
        conv_x_w[:, 0],
        conv_x_bias[0],
        start_at,
        segment,
        positions,
        lagged,
    )
    bc_conv = convolve(
        bc_raw,
        prior_bc,
        bc_edges,
        lax.dynamic_slice_in_dim(conv_bc_w[:, 0], row_at * bc_cols, bc_cols, axis=1),
        lax.dynamic_slice_in_dim(conv_bc_bias[0], row_at * bc_cols, bc_cols, axis=0),
        start_at,
        segment,
        positions,
        lagged,
    )
    x_heads = x_conv.reshape(rows_here, heads_here, P_SIZE)
    bc_swapped = lax.ppermute(bc_conv, "row", [(0, 1), (1, 0)])
    bc_conv = jnp.concatenate(
        [jnp.where(row_first, bc_conv, bc_swapped), jnp.where(row_first, bc_swapped, bc_conv)], axis=1
    )
    b_proj = bc_conv[:, :N]
    c_proj = bc_conv[:, N:]
    dt_vals = jax.nn.softplus(dt_raw.astype(jnp.float32) + dt_bias[0][None, :])
    init_vals = init_states[:, 0]
    y_part, carried, seg_ends, decay_all, state_add, end_zero, started = local_terms(
        x_heads, b_proj, c_proj, dt_vals, flag_vals, init_vals, decay_rate[0]
    )

    seq_count = lax.axis_size("seq")
    seq_at = lax.axis_index("seq")
    heads_n, p_n, n_n = state_add.shape
    ones = jnp.ones((heads_n,), jnp.float32)
    zeros_state = jnp.zeros_like(state_add)
    has_start = jnp.where(started > 0, 1.0, 0.0).astype(jnp.float32)

    def pack(decay, state, mark):
        aux = jnp.concatenate(
            [
                jnp.broadcast_to(decay[:, None], (heads_n, n_n // 2)),
                jnp.broadcast_to(mark, (heads_n, n_n - n_n // 2)),
            ],
            axis=1,
        )
        return jnp.concatenate([state, aux[:, None, :]], axis=1)

    def unpack(packed):
        return packed[:, p_n, 0], packed[:, :p_n], packed[0, p_n, n_n - 1]

    fwd_in = (decay_all * ones, state_add)
    fwd_ex = (ones, zeros_state)
    bwd_in = (jnp.exp(end_zero), seg_ends[0], has_start)
    bwd_ex = (ones, zeros_state, jnp.zeros((), jnp.float32))
    shift = 1
    while shift < seq_count:
        last = 2 * shift >= seq_count
        got_f = from_behind(pack(fwd_in[0], fwd_in[1], 0.0), "seq", shift)
        got_b = from_behind(pack(*bwd_in), "seq", -shift)
        early_a, early_b, _ = unpack(got_f)
        late_a, late_b, late_m = unpack(got_b)
        late_ok = seq_at + shift < seq_count
        fwd_ex = (
            fwd_ex[0] * early_a,
            fwd_ex[0][:, None, None] * early_b + fwd_ex[1],
        )

        def near_far(near, far_a, far_b, far_m):
            keep = (near[2] > 0.5) | jnp.logical_not(late_ok)
            return (
                jnp.where(keep, near[0], far_a * near[0]),
                jnp.where(keep, near[1], far_a[:, None, None] * near[1] + far_b),
                jnp.where(keep, near[2], far_m),
            )

        bwd_ex = near_far(bwd_ex, late_a, late_b, late_m)
        if not last:
            fwd_in = (
                fwd_in[0] * early_a,
                fwd_in[0][:, None, None] * early_b + fwd_in[1],
            )
            bwd_in = near_far(bwd_in, late_a, late_b, late_m)
        fwd_in, fwd_ex, bwd_in, bwd_ex = lax.optimization_barrier((fwd_in, fwd_ex, bwd_in, bwd_ex))
        shift *= 2
    state_in = fwd_ex[1]
    carried_in = jnp.einsum("tn,hpn->thp", c_proj.astype(jnp.float32), state_in, precision=PRECISE)
    y_full = (
        y_part
        + carried[:, :, None] * carried_in
        + d_skip[0][None, :, None] * x_heads.astype(jnp.float32)
    )
    tail_state = bwd_ex[0][:, None, None] * state_add + bwd_ex[1]
    slot_ids = jnp.arange(1, init_vals.shape[0] + 1, dtype=jnp.int32)
    finals = jnp.where(
        (slot_ids < started)[:, None, None, None],
        seg_ends[1:],
        jnp.where((slot_ids == started)[:, None, None, None], tail_state[None], 0.0),
    )
    gated = y_full.reshape(rows_here, channels) * jax.nn.silu(z_gate.astype(jnp.float32))
    partial_sq = jnp.sum(gated * gated, axis=-1)
    total_sq = lax.psum(partial_sq, "row")
    mean_sq = total_sq / (channels * lax.axis_size("row"))
    gated_out = (gated * lax.rsqrt(mean_sq + EPSILON)[:, None] * norm_gain[0][None, :]).astype(
        jnp.bfloat16
    )
    return (gated_out.reshape(rows_here, 1, channels), finals[:, None])


def solution(mesh):
    placed = (
        P(("seq", "row"), "col"),
        P("col", None, "row"),
        P("col", None, "row"),
        P("col", None, None),
        P("col", None, "row"),
        P(None, "col", "row"),
        P(None, "col", None),
        P("col", "row"),
        P("col", None),
        P("col", "row"),
        P("col", "row"),
        P("col", "row"),
        P("col", "row"),
        P("seq"),
        P("seq", "col", "row", None, None),
        P("seq", None, "col", "row"),
        P("seq", None, "col", None),
    )
    return jax.shard_map(
        shards,
        mesh=mesh,
        in_specs=placed,
        out_specs=(P("seq", "col", "row"), P("seq", "col", "row", None, None)),
        check_vma=False,
    )
```

```python
import jax
import jax.numpy as jnp
from jax import lax
from jax.sharding import PartitionSpec as P

P_SIZE = 64
N = 128


PRECISE = lax.Precision.HIGHEST
EPSILON = 1e-05


def from_behind(value, axis, steps):
    count = lax.axis_size(axis)
    first, last = (max(0, -steps), min(count, count - steps))
    return lax.ppermute(value, axis, [(source, source + steps) for source in range(first, last)])


def local_terms(x_vals, b_proj, c_proj, dt_vals, flag_vals, init_vals, rate_vals):
    rows_here = x_vals.shape[0]
    slot_total = init_vals.shape[0]
    positions = jnp.arange(rows_here, dtype=jnp.int32)
    segment = jnp.cumsum(flag_vals.astype(jnp.int32))
    started = segment[rows_here - 1]
    log_decay = -dt_vals * rate_vals[None, :]
    cumulative = jnp.cumsum(log_decay, axis=0)
    preceding = cumulative - log_decay
    start_at = lax.cummax(jnp.where(flag_vals, positions, 0), axis=0)
    baseline = jnp.where((segment > 0)[:, None], preceding[start_at], 0.0)
    joined = (segment[:, None] == segment[None, :]) & (positions[:, None] >= positions[None, :])
    intersection = jnp.dot(c_proj, b_proj.T, preferred_element_type=jnp.float32)
    cumul_t = cumulative.T
    spread = jnp.where(joined[None], cumul_t[:, :, None] - cumul_t[:, None, :], 0.0)
    mixing = (
        jnp.where(joined[None], jnp.exp(spread), 0.0) * intersection[None] * dt_vals.T[:, None, :]
    )
    internal = jnp.einsum("hij,jhp->ihp", mixing, x_vals.astype(jnp.float32), precision=PRECISE)
    from_slot = jnp.einsum(
        "tn,shpn->tshp", c_proj.astype(jnp.float32), init_vals, precision=PRECISE
    )
    slot_ids = jnp.arange(1, slot_total + 1, dtype=jnp.int32)
    chosen = (segment[:, None] == slot_ids[None, :]).astype(jnp.float32)
    restarted = jnp.einsum("ts,tshp->thp", chosen, from_slot, precision=PRECISE)
    y_part = internal + jnp.exp(cumulative - baseline)[:, :, None] * restarted
    carried = jnp.where((segment == 0)[:, None], jnp.exp(cumulative), 0.0)
    indices = jnp.arange(slot_total + 1, dtype=jnp.int32)
    belongs = segment[:, None] == indices[None, :]
    last_at = jnp.max(jnp.where(belongs, positions[:, None], -1), axis=0)
    first_at = jnp.min(jnp.where(belongs, positions[:, None], rows_here), axis=0)
    cumul_end = jnp.where((last_at >= 0)[:, None], cumulative[jnp.maximum(last_at, 0)], 0.0)
    lag_spread = jnp.where(belongs.T[:, :, None], cumul_end[:, None, :] - cumulative[None], 0.0)
    weights = jnp.where(belongs.T[:, :, None], jnp.exp(lag_spread), 0.0) * dt_vals[None]
    weighted = weights[..., None] * x_vals.astype(jnp.float32)[None]
    gathered = jnp.einsum("sthp,tn->shpn", weighted, b_proj.astype(jnp.float32), precision=PRECISE)
    base_slot = preceding[jnp.minimum(first_at, rows_here - 1)]
    factor = jnp.exp(jnp.where((slot_ids <= started)[:, None], cumul_end[1:] - base_slot[1:], 0.0))
    in_use = slot_ids <= started
    seg_rest = gathered[1:] + jnp.where(
        in_use[:, None, None, None], factor[..., None, None] * init_vals, 0.0
    )
    seg_ends = jnp.concatenate([gathered[:1], seg_rest], axis=0)
    decay_all = jnp.where(started == 0, jnp.exp(cumulative[rows_here - 1]), 0.0)
    state_add = jnp.sum(jnp.where((indices == started)[:, None, None, None], seg_ends, 0.0), axis=0)
    return (y_part, carried, seg_ends, decay_all, state_add, cumul_end[0], started)


def tail_rows(raw, edges, start_last, segment_last, lagged):
    rows_here = raw.shape[0]
    source = jnp.arange(rows_here - lagged, rows_here, dtype=jnp.int32)
    inside = source >= start_last
    row_pick = jnp.clip(lagged - start_last + source, 0, lagged - 1)
    from_edge = edges[jnp.maximum(segment_last - 1, 0), row_pick]
    return jnp.where(inside[:, None], raw[rows_here - lagged :], from_edge)


def convolve(raw, prior, edges, kernel, offset_bias, start_at, segment, positions, lagged):
    rows_here = raw.shape[0]
    slot_total = edges.shape[0]
    extended = jnp.concatenate([prior, raw], axis=0)
    table = edges.reshape(slot_total * lagged, edges.shape[-1])
    total = offset_bias[None].astype(jnp.float32) + kernel[lagged][None].astype(
        jnp.float32
    ) * raw.astype(jnp.float32)
    for offset in range(1, lagged + 1):
        source = positions - offset
        inside = source >= start_at
        row_pick = jnp.clip(lagged - start_at + source, 0, lagged - 1)
        which = jnp.maximum(segment - 1, 0) * lagged + row_pick
        picker = (
            which[:, None] == jnp.arange(slot_total * lagged, dtype=jnp.int32)[None, :]
        ).astype(jnp.bfloat16)
        from_edge = jnp.dot(picker, table, preferred_element_type=jnp.float32)
        earlier = extended[lagged - offset : lagged - offset + rows_here].astype(jnp.float32)
        total = total + kernel[lagged - offset][None].astype(jnp.float32) * jnp.where(
            inside[:, None], earlier, from_edge
        )
    return jax.nn.silu(total).astype(jnp.bfloat16)


def shards(
    hidden,
    w_x,
    w_z,
    w_bc,
    w_dt,
    conv_x_w,
    conv_bc_w,
    conv_x_bias,
    conv_bc_bias,
    dt_bias,
    decay_rate,
    d_skip,
    norm_gain,
    starts,
    init_states,
    conv_x_edges,
    conv_bc_edges,
):
    other = lax.ppermute(hidden, "row", [(0, 1), (1, 0)])
    row_first = lax.axis_index("row") == 0
    tokens = jnp.concatenate(
        [jnp.where(row_first, hidden, other), jnp.where(row_first, other, hidden)], axis=0
    )
    rows_here = tokens.shape[0]
    channels = w_x.shape[2]
    heads_here = w_dt.shape[2]
    lagged = conv_x_w.shape[0] - 1
    row_at = lax.axis_index("row")
    bc_cols = w_bc.shape[2] // lax.axis_size("row")
    w_bc_mine = lax.dynamic_slice_in_dim(w_bc, row_at * bc_cols, bc_cols, axis=2)
    x_part, z_part, bc_part, dt_part = [
        jnp.einsum("td,dgc->gtc", tokens, weight, preferred_element_type=jnp.float32)
        for weight in (w_x, w_z, w_bc_mine, w_dt)
    ]
    first = lax.psum_scatter(
        jnp.concatenate([x_part, bc_part, dt_part], axis=2), "col", scatter_dimension=0, tiled=True
    )[0].astype(jnp.bfloat16)
    first, z_part = lax.optimization_barrier((first, z_part))
    z_gate = lax.optimization_barrier(
        lax.psum_scatter(z_part, "col", scatter_dimension=0, tiled=True)[0].astype(jnp.bfloat16)
    )
    x_raw = first[:, :channels]
    bc_mine = first[:, channels : channels + bc_cols]
    bc_other = lax.ppermute(bc_mine, "row", [(0, 1), (1, 0)])
    bc_raw = jnp.concatenate(
        [jnp.where(row_first, bc_mine, bc_other), jnp.where(row_first, bc_other, bc_mine)], axis=1
    )
    dt_raw = first[:, channels + bc_cols :]
    positions = jnp.arange(rows_here, dtype=jnp.int32)
    flag_vals = starts == 1
    segment = jnp.cumsum(starts)
    start_at = lax.cummax(jnp.where(flag_vals, positions, -lagged), axis=0)
    x_edges = conv_x_edges[:, :, 0]
    bc_edges = conv_bc_edges[:, :, 0]
    start_last = start_at[rows_here - 1]
    segment_last = segment[rows_here - 1]
    send_x = tail_rows(x_raw, x_edges, start_last, segment_last, lagged)
    send_bc = tail_rows(bc_raw, bc_edges, start_last, segment_last, lagged)
    prior_both = from_behind(jnp.concatenate([send_x, send_bc], axis=1), "seq", 1)
    prior_x = prior_both[:, :channels]
    prior_bc = prior_both[:, channels:]
    x_conv = convolve(
        x_raw,
        prior_x,
        x_edges,
        conv_x_w[:, 0],
        conv_x_bias[0],
        start_at,
        segment,
        positions,
        lagged,
    )
    bc_conv = convolve(
        bc_raw,
        prior_bc,
        bc_edges,
        conv_bc_w[:, 0],
        conv_bc_bias[0],
        start_at,
        segment,
        positions,
        lagged,
    )
    x_heads = x_conv.reshape(rows_here, heads_here, P_SIZE)
    b_proj = bc_conv[:, :N]
    c_proj = bc_conv[:, N:]
    dt_vals = jax.nn.softplus(dt_raw.astype(jnp.float32) + dt_bias[0][None, :])
    init_vals = init_states[:, 0]
    y_part, carried, seg_ends, decay_all, state_add, end_zero, started = local_terms(
        x_heads, b_proj, c_proj, dt_vals, flag_vals, init_vals, decay_rate[0]
    )

    seq_count = lax.axis_size("seq")
    seq_at = lax.axis_index("seq")
    heads_n, p_n, n_n = state_add.shape
    ones = jnp.ones((heads_n,), jnp.float32)
    zeros_state = jnp.zeros_like(state_add)
    has_start = jnp.where(started > 0, 1.0, 0.0).astype(jnp.float32)

    def pack(decay, state, mark):
        aux = jnp.concatenate(
            [
                jnp.broadcast_to(decay[:, None], (heads_n, n_n // 2)),
                jnp.broadcast_to(mark, (heads_n, n_n - n_n // 2)),
            ],
            axis=1,
        )
        return jnp.concatenate([state, aux[:, None, :]], axis=1)

    row_ids = jnp.arange(p_n + 1, dtype=jnp.int32)[None, :, None]
    lane_ids = jnp.arange(n_n, dtype=jnp.int32)[None, None, :]
    keep_b = (row_ids < p_n).astype(jnp.float32)
    keep_bm = ((row_ids < p_n) | (lane_ids >= n_n // 2)).astype(jnp.float32)

    def decay_of(packed):
        return packed[:, p_n, 0][:, None, None]

    fwd_in = pack(decay_all * ones, state_add, 0.0)
    fwd_ex = pack(ones, zeros_state, 0.0)
    bwd_in = pack(jnp.exp(end_zero), seg_ends[0], has_start)
    bwd_ex = pack(ones, zeros_state, 0.0)
    shift = 1
    while shift < seq_count:
        last = 2 * shift >= seq_count
        got_f = from_behind(fwd_in, "seq", shift)
        got_b = from_behind(bwd_in, "seq", -shift)
        late_ok = seq_at + shift < seq_count
        fwd_ex = decay_of(fwd_ex) * got_f + fwd_ex * keep_b

        def near_far(near):
            keep = (near[0, p_n, n_n - 1] > 0.5) | jnp.logical_not(late_ok)
            return jnp.where(keep, near, decay_of(got_b) * near + got_b * keep_bm)

        bwd_ex = near_far(bwd_ex)
        if not last:
            fwd_in = decay_of(fwd_in) * got_f + fwd_in * keep_b
            bwd_in = near_far(bwd_in)
        fwd_in, fwd_ex, bwd_in, bwd_ex = lax.optimization_barrier((fwd_in, fwd_ex, bwd_in, bwd_ex))
        shift *= 2
    state_in = fwd_ex[:, :p_n]
    carried_in = jnp.einsum("tn,hpn->thp", c_proj.astype(jnp.float32), state_in, precision=PRECISE)
    y_full = (
        y_part
        + carried[:, :, None] * carried_in
        + d_skip[0][None, :, None] * x_heads.astype(jnp.float32)
    )
    tail_state = decay_of(bwd_ex) * state_add + bwd_ex[:, :p_n]
    slot_ids = jnp.arange(1, init_vals.shape[0] + 1, dtype=jnp.int32)
    finals = jnp.where(
        (slot_ids < started)[:, None, None, None],
        seg_ends[1:],
        jnp.where((slot_ids == started)[:, None, None, None], tail_state[None], 0.0),
    )
    gated = y_full.reshape(rows_here, channels) * jax.nn.silu(z_gate.astype(jnp.float32))
    partial_sq = jnp.sum(gated * gated, axis=-1)
    total_sq = lax.psum(partial_sq, "row")
    mean_sq = total_sq / (channels * lax.axis_size("row"))
    gated_out = (gated * lax.rsqrt(mean_sq + EPSILON)[:, None] * norm_gain[0][None, :]).astype(
        jnp.bfloat16
    )
    return (gated_out.reshape(rows_here, 1, channels), finals[:, None])


def solution(mesh):
    placed = (
        P(("seq", "row"), "col"),
        P("col", None, "row"),
        P("col", None, "row"),
        P("col", None, None),
        P("col", None, "row"),
        P(None, "col", "row"),
        P(None, "col", None),
        P("col", "row"),
        P("col", None),
        P("col", "row"),
        P("col", "row"),
        P("col", "row"),
        P("col", "row"),
        P("seq"),
        P("seq", "col", "row", None, None),
        P("seq", None, "col", "row"),
        P("seq", None, "col", None),
    )
    return jax.shard_map(
        shards,
        mesh=mesh,
        in_specs=placed,
        out_specs=(P("seq", "col", "row"), P("seq", "col", "row", None, None)),
        check_vma=False,
    )
```

```python
import jax
import jax.numpy as jnp
from jax import lax
from jax.sharding import PartitionSpec as P

P_SIZE = 64
N = 128


PRECISE = lax.Precision.HIGHEST
EPSILON = 1e-05


def from_behind(value, axis, steps):
    count = lax.axis_size(axis)
    first, last = (max(0, -steps), min(count, count - steps))
    return lax.ppermute(value, axis, [(source, source + steps) for source in range(first, last)])


def local_terms(x_vals, b_proj, c_proj, dt_vals, flag_vals, init_vals, rate_vals):
    rows_here = x_vals.shape[0]
    slot_total = init_vals.shape[0]
    positions = jnp.arange(rows_here, dtype=jnp.int32)
    segment = jnp.cumsum(flag_vals.astype(jnp.int32))
    started = segment[rows_here - 1]
    log_decay = -dt_vals * rate_vals[None, :]
    cumulative = jnp.cumsum(log_decay, axis=0)
    preceding = cumulative - log_decay
    start_at = lax.cummax(jnp.where(flag_vals, positions, 0), axis=0)
    baseline = jnp.where((segment > 0)[:, None], preceding[start_at], 0.0)
    joined = (segment[:, None] == segment[None, :]) & (positions[:, None] >= positions[None, :])
    intersection = jnp.dot(c_proj, b_proj.T, preferred_element_type=jnp.float32)
    cumul_t = cumulative.T
    spread = jnp.where(joined[None], cumul_t[:, :, None] - cumul_t[:, None, :], 0.0)
    mixing = (
        jnp.where(joined[None], jnp.exp(spread), 0.0) * intersection[None] * dt_vals.T[:, None, :]
    )
    internal = jnp.einsum("hij,jhp->ihp", mixing, x_vals.astype(jnp.float32), precision=PRECISE)
    from_slot = jnp.einsum(
        "tn,shpn->tshp", c_proj.astype(jnp.float32), init_vals, precision=PRECISE
    )
    slot_ids = jnp.arange(1, slot_total + 1, dtype=jnp.int32)
    chosen = (segment[:, None] == slot_ids[None, :]).astype(jnp.float32)
    restarted = jnp.einsum("ts,tshp->thp", chosen, from_slot, precision=PRECISE)
    y_part = internal + jnp.exp(cumulative - baseline)[:, :, None] * restarted
    carried = jnp.where((segment == 0)[:, None], jnp.exp(cumulative), 0.0)
    indices = jnp.arange(slot_total + 1, dtype=jnp.int32)
    belongs = segment[:, None] == indices[None, :]
    last_at = jnp.max(jnp.where(belongs, positions[:, None], -1), axis=0)
    first_at = jnp.min(jnp.where(belongs, positions[:, None], rows_here), axis=0)
    cumul_end = jnp.where((last_at >= 0)[:, None], cumulative[jnp.maximum(last_at, 0)], 0.0)
    lag_spread = jnp.where(belongs.T[:, :, None], cumul_end[:, None, :] - cumulative[None], 0.0)
    weights = jnp.where(belongs.T[:, :, None], jnp.exp(lag_spread), 0.0) * dt_vals[None]
    weighted = weights[..., None] * x_vals.astype(jnp.float32)[None]
    gathered = jnp.einsum("sthp,tn->shpn", weighted, b_proj.astype(jnp.float32), precision=PRECISE)
    base_slot = preceding[jnp.minimum(first_at, rows_here - 1)]
    factor = jnp.exp(jnp.where((slot_ids <= started)[:, None], cumul_end[1:] - base_slot[1:], 0.0))
    in_use = slot_ids <= started
    seg_rest = gathered[1:] + jnp.where(
        in_use[:, None, None, None], factor[..., None, None] * init_vals, 0.0
    )
    seg_ends = jnp.concatenate([gathered[:1], seg_rest], axis=0)
    decay_all = jnp.where(started == 0, jnp.exp(cumulative[rows_here - 1]), 0.0)
    state_add = jnp.sum(jnp.where((indices == started)[:, None, None, None], seg_ends, 0.0), axis=0)
    return (y_part, carried, seg_ends, decay_all, state_add, cumul_end[0], started)


def tail_rows(raw, edges, start_last, segment_last, lagged):
    rows_here = raw.shape[0]
    source = jnp.arange(rows_here - lagged, rows_here, dtype=jnp.int32)
    inside = source >= start_last
    row_pick = jnp.clip(lagged - start_last + source, 0, lagged - 1)
    from_edge = edges[jnp.maximum(segment_last - 1, 0), row_pick]
    return jnp.where(inside[:, None], raw[rows_here - lagged :], from_edge)


def convolve(raw, prior, edges, kernel, offset_bias, start_at, segment, positions, lagged):
    rows_here = raw.shape[0]
    slot_total = edges.shape[0]
    extended = jnp.concatenate([prior, raw], axis=0)
    table = edges.reshape(slot_total * lagged, edges.shape[-1])
    total = offset_bias[None].astype(jnp.float32) + kernel[lagged][None].astype(
        jnp.float32
    ) * raw.astype(jnp.float32)
    for offset in range(1, lagged + 1):
        source = positions - offset
        inside = source >= start_at
        row_pick = jnp.clip(lagged - start_at + source, 0, lagged - 1)
        which = jnp.maximum(segment - 1, 0) * lagged + row_pick
        picker = (
            which[:, None] == jnp.arange(slot_total * lagged, dtype=jnp.int32)[None, :]
        ).astype(jnp.bfloat16)
        from_edge = jnp.dot(picker, table, preferred_element_type=jnp.float32)
        earlier = extended[lagged - offset : lagged - offset + rows_here].astype(jnp.float32)
        total = total + kernel[lagged - offset][None].astype(jnp.float32) * jnp.where(
            inside[:, None], earlier, from_edge
        )
    return jax.nn.silu(total).astype(jnp.bfloat16)


def shards(
    hidden,
    w_x,
    w_z,
    w_bc,
    w_dt,
    conv_x_w,
    conv_bc_w,
    conv_x_bias,
    conv_bc_bias,
    dt_bias,
    decay_rate,
    d_skip,
    norm_gain,
    starts,
    init_states,
    conv_x_edges,
    conv_bc_edges,
):
    other = lax.ppermute(hidden, "row", [(0, 1), (1, 0)])
    row_first = lax.axis_index("row") == 0
    tokens = jnp.concatenate(
        [jnp.where(row_first, hidden, other), jnp.where(row_first, other, hidden)], axis=0
    )
    rows_here = tokens.shape[0]
    channels = w_x.shape[2]
    heads_here = w_dt.shape[2]
    lagged = conv_x_w.shape[0] - 1
    row_at = lax.axis_index("row")
    bc_cols = w_bc.shape[2] // lax.axis_size("row")
    w_bc_mine = lax.dynamic_slice_in_dim(w_bc, row_at * bc_cols, bc_cols, axis=2)
    x_part, z_part, bc_part, dt_part = [
        jnp.einsum("td,dgc->gtc", tokens, weight, preferred_element_type=jnp.float32)
        for weight in (w_x, w_z, w_bc_mine, w_dt)
    ]
    first = lax.psum_scatter(
        jnp.concatenate([x_part, bc_part, dt_part], axis=2), "col", scatter_dimension=0, tiled=True
    )[0].astype(jnp.bfloat16)
    first, z_part = lax.optimization_barrier((first, z_part))
    z_gate = lax.optimization_barrier(
        lax.psum_scatter(z_part, "col", scatter_dimension=0, tiled=True)[0].astype(jnp.bfloat16)
    )
    x_raw = first[:, :channels]
    bc_mine = first[:, channels : channels + bc_cols]
    bc_other = lax.ppermute(bc_mine, "row", [(0, 1), (1, 0)])
    bc_raw = jnp.concatenate(
        [jnp.where(row_first, bc_mine, bc_other), jnp.where(row_first, bc_other, bc_mine)], axis=1
    )
    dt_raw = first[:, channels + bc_cols :]
    positions = jnp.arange(rows_here, dtype=jnp.int32)
    flag_vals = starts == 1
    segment = jnp.cumsum(starts)
    start_at = lax.cummax(jnp.where(flag_vals, positions, -lagged), axis=0)
    x_edges = conv_x_edges[:, :, 0]
    bc_edges = conv_bc_edges[:, :, 0]
    start_last = start_at[rows_here - 1]
    segment_last = segment[rows_here - 1]
    send_x = tail_rows(x_raw, x_edges, start_last, segment_last, lagged)
    send_bc = tail_rows(bc_raw, bc_edges, start_last, segment_last, lagged)
    prior_both = from_behind(jnp.concatenate([send_x, send_bc], axis=1), "seq", 1)
    prior_x = prior_both[:, :channels]
    prior_bc = prior_both[:, channels:]
    x_conv = convolve(
        x_raw,
        prior_x,
        x_edges,
        conv_x_w[:, 0],
        conv_x_bias[0],
        start_at,
        segment,
        positions,
        lagged,
    )
    bc_conv = convolve(
        bc_raw,
        prior_bc,
        bc_edges,
        conv_bc_w[:, 0],
        conv_bc_bias[0],
        start_at,
        segment,
        positions,
        lagged,
    )
    x_heads = x_conv.reshape(rows_here, heads_here, P_SIZE)
    b_proj = bc_conv[:, :N]
    c_proj = bc_conv[:, N:]
    dt_vals = jax.nn.softplus(dt_raw.astype(jnp.float32) + dt_bias[0][None, :])
    init_vals = init_states[:, 0]
    y_part, carried, seg_ends, decay_all, state_add, end_zero, started = local_terms(
        x_heads, b_proj, c_proj, dt_vals, flag_vals, init_vals, decay_rate[0]
    )

    seq_count = lax.axis_size("seq")
    seq_at = lax.axis_index("seq")
    heads_n, p_n, n_n = state_add.shape
    ones = jnp.ones((heads_n,), jnp.float32)
    zeros_state = jnp.zeros_like(state_add)
    has_start = jnp.where(started > 0, 1.0, 0.0).astype(jnp.float32)

    def pack(decay, state, mark):
        aux = jnp.concatenate(
            [
                jnp.broadcast_to(decay[:, None], (heads_n, n_n // 2)),
                jnp.broadcast_to(mark, (heads_n, n_n - n_n // 2)),
            ],
            axis=1,
        )
        return jnp.concatenate([state, aux[:, None, :]], axis=1)

    def unpack(packed):
        return packed[:, p_n, 0], packed[:, :p_n], packed[0, p_n, n_n - 1]

    fwd_in = (decay_all * ones, state_add)
    fwd_ex = (ones, zeros_state)
    bwd_in = (jnp.exp(end_zero), seg_ends[0], has_start)
    bwd_ex = (ones, zeros_state, jnp.zeros((), jnp.float32))
    shift = 1
    while shift < seq_count:
        last = 2 * shift >= seq_count
        got_f = from_behind(pack(fwd_in[0], fwd_in[1], 0.0), "seq", shift)
        got_b = from_behind(pack(*bwd_in), "seq", -shift)
        early_a, early_b, _ = unpack(got_f)
        late_a, late_b, late_m = unpack(got_b)
        late_ok = seq_at + shift < seq_count
        fwd_ex = (
            fwd_ex[0] * early_a,
            fwd_ex[0][:, None, None] * early_b + fwd_ex[1],
        )

        def near_far(near, far_a, far_b, far_m):
            keep = (near[2] > 0.5) | jnp.logical_not(late_ok)
            return (
                jnp.where(keep, near[0], far_a * near[0]),
                jnp.where(keep, near[1], far_a[:, None, None] * near[1] + far_b),
                jnp.where(keep, near[2], far_m),
            )

        bwd_ex = near_far(bwd_ex, late_a, late_b, late_m)
        if not last:
            fwd_in = (
                fwd_in[0] * early_a,
                fwd_in[0][:, None, None] * early_b + fwd_in[1],
            )
            bwd_in = near_far(bwd_in, late_a, late_b, late_m)
        fwd_in, fwd_ex, bwd_in, bwd_ex = lax.optimization_barrier((fwd_in, fwd_ex, bwd_in, bwd_ex))
        shift *= 2
    state_in = fwd_ex[1]
    carried_in = jnp.einsum("tn,hpn->thp", c_proj.astype(jnp.float32), state_in, precision=PRECISE)
    y_full = (
        y_part
        + carried[:, :, None] * carried_in
        + d_skip[0][None, :, None] * x_heads.astype(jnp.float32)
    )
    tail_state = bwd_ex[0][:, None, None] * state_add + bwd_ex[1]
    slot_ids = jnp.arange(1, init_vals.shape[0] + 1, dtype=jnp.int32)
    finals = jnp.where(
        (slot_ids < started)[:, None, None, None],
        seg_ends[1:],
        jnp.where((slot_ids == started)[:, None, None, None], tail_state[None], 0.0),
    )
    gated = y_full.reshape(rows_here, channels) * jax.nn.silu(z_gate.astype(jnp.float32))
    partial_sq = jnp.sum(gated * gated, axis=-1)
    total_sq = partial_sq + lax.ppermute(partial_sq, "row", [(0, 1), (1, 0)])
    mean_sq = total_sq / (channels * lax.axis_size("row"))
    gated_out = (gated * lax.rsqrt(mean_sq + EPSILON)[:, None] * norm_gain[0][None, :]).astype(
        jnp.bfloat16
    )
    return (gated_out.reshape(rows_here, 1, channels), finals[:, None])


def solution(mesh):
    placed = (
        P(("seq", "row"), "col"),
        P("col", None, "row"),
        P("col", None, "row"),
        P("col", None, None),
        P("col", None, "row"),
        P(None, "col", "row"),
        P(None, "col", None),
        P("col", "row"),
        P("col", None),
        P("col", "row"),
        P("col", "row"),
        P("col", "row"),
        P("col", "row"),
        P("seq"),
        P("seq", "col", "row", None, None),
        P("seq", None, "col", "row"),
        P("seq", None, "col", None),
    )
    return jax.shard_map(
        shards,
        mesh=mesh,
        in_specs=placed,
        out_specs=(P("seq", "col", "row"), P("seq", "col", "row", None, None)),
        check_vma=False,
    )
```
